128 devices in a mesh: req: 4 (over y), exp: 32 (over z, x, core).
Axes of the slice: x: 4, y: 4, z: 4, core: 2. Of those that a mesh axis runs over, the one named last changes fastest.
Arguments:
- states: bfloat16 [2, 16384, 1024], P(None, ('req', 'exp')), may hold values from -6 to 6
- lengths: int32 [128, 4], P(('req', 'exp')), may hold values from 1 to 64, 128 in all within a row
- targets: int32 [16384], P('req'), may hold values from 0 to 36863
- routes: int32 [2, 16384, 8], P(None, ('req', 'exp')), may hold values from 0 to 31, all different within a row; in each aligned block of 128 rows (0 to 127, 128 to 255, ..., all dimensions but the last counted through in order) at most 40 rows name the same one
- gate_probs: float32 [2, 16384, 8], P(None, ('req', 'exp')), may hold values from 0.02 to 0.4
- owners: int32 [512], P(('req', 'exp')), may hold values from 0 to 511, each once
- norm_gains: float32 [2, 3, 1024], replicated, may hold values from 0.25 to 1.75
- qkv_weight: bfloat16 [2, 1024, 2048], replicated, may hold values from -14 to 14
- out_weight: bfloat16 [2, 1024, 1024], replicated, may hold values from -0.1875 to 0.1875
- expert_in: bfloat16 [2, 32, 1024, 1024], P(None, 'exp'), may hold values from -0.1875 to 0.1875
- expert_down: bfloat16 [2, 32, 512, 1024], P(None, 'exp'), may hold values from -0.25 to 0.25
- vocab_head: bfloat16 [2, 36864, 1024], P(None, 'exp'), may hold values from -170 to 170
Outputs:
- token_logp: float32 [2, 16384], P(None, ('req', 'exp'))
- seq_totals: float32 [512], P(('req', 'exp'))
The draws below stay inside these ranges and needn't reach their ends.
Inputs may be any that keep to these rules, and one draw needn't show every extreme that they name: `lengths`: each row sums to 128; some row reaches 64. `routes`: the 8 experts of a token are distinct; among the 128 tokens of one device, no expert is named by more than 40 of them for one model, and that bound is reached. `owners`: a permutation of the sequence numbers.
All inputs are finite; a program needn't handle non-finite values.
Results may differ from the reference program's by a relative error of at most 0.012.
The reference program's roundings to bfloat16 on the way count: a program that leaves them out, or rounds other values in their place, can miss the bound.
Values may be sent and summed in bfloat16 or wider, within the bound.
No kernel may reach another device: no remote copies, remote signals or barrier semaphores. Data moves between devices by JAX's collectives and lax.ppermute only.
A program may use at most 128 MiB of HBM per device.

```python
import math
import jax
import jax.numpy as jnp
import numpy as np
from jax import lax

D = 1024
HEADS = 16
KV_HEADS = 8
HEAD_DIM = 64
EXPERT_FF = 512
EXPERTS = 32
TOP = 8
TOK_DEV = 128
SEQ_DEV = 4
CAP = 40
LEN_MAX = 64
TOKENS = 16384
SEQUENCES = 512
VOCAB = 36864
N_REQ = 4
N_EXP = 32


def draw_qkv_weight(key, part):
    width = (HEADS + 2 * KV_HEADS) * HEAD_DIM
    values = jnp.clip(jax.random.normal(jax.random.fold_in(key, 11), (2, D, width), jnp.float32), -6.0, 6.0) / math.sqrt(D)
    return values.astype(jnp.bfloat16)


def draw_vocab_head(key, part):
    values = jnp.clip(jax.random.normal(jax.random.fold_in(key, 21), (2, VOCAB, D), jnp.float32), -6.0, 6.0) * (18.0 / math.sqrt(D))
    return values.astype(jnp.bfloat16)


def plant(values, stream_key, smallest, largest):
    index_at = [jax.random.randint(jax.random.fold_in(stream_key, axis), (), 0, length) for axis, length in enumerate(values.shape)]
    longest = values.shape.index(max(values.shape))
    next_to = index_at[:longest] + [(index_at[longest] + 1) % values.shape[longest]] + index_at[longest + 1:]
    return values.at[tuple(index_at)].set(smallest).at[tuple(next_to)].set(largest)


def shard_levels(stream_key, dims, cuts, smallest, high):
    def one(dim, blocks):
        heights = jax.random.uniform(jax.random.fold_in(jax.random.fold_in(stream_key, 6), dim), (blocks,), jnp.float32, smallest / len(cuts), high / len(cuts))
        return jnp.repeat(jnp.exp(heights), dims[dim] // blocks).reshape((-1,) + (1,) * (len(dims) - dim - 1))

    gain = one(*cuts[0])
    for cut in cuts[1:]:
        gain = gain * one(*cut)
    return gain


def rank_bounds(amount, skew):
    weights = [(1 << 20) // math.isqrt(grade ** skew) + 1 for grade in range(1, amount + 1)]
    spread = 1 + sum(weights) // (1 << 30)
    return np.cumsum(np.array([max(1, weight // spread) for weight in weights]))


def ranked_ids(rng, extent, amount, skew):
    listing = rank_bounds(amount, skew)
    ticket = jax.random.randint(jax.random.fold_in(rng, 1), extent, 0, int(listing[amount - 1]))
    rank = jnp.searchsorted(jnp.asarray(listing, jnp.int32), ticket, side="right")
    return jax.random.permutation(jax.random.fold_in(rng, 2), amount)[rank].astype(jnp.int32)


def length_profile(count, total, bound, lean):
    portions = [(1 << 20) // math.isqrt(rank ** lean) + 1 for rank in range(2, count + 1)]
    rest, given = total - bound - (count - 1), [1] * (count - 1)
    while rest > 0:
        candidates = [i for i in range(count - 1) if given[i] < bound]
        mass, remaining = sum([portions[i] for i in candidates]), rest
        for i in candidates:
            more = min(bound - given[i], max(1, remaining * portions[i] // mass), rest)
            given[i] = given[i] + more
            rest = rest - more
    return np.array([bound] + given)


def ragged(key, count, total, most, slope):
    if count == 2:
        one = jax.random.randint(key, (), max(1, total - most), min(most, total - 1) + 1)
        return jnp.stack([one, total - one])
    tallies = jnp.asarray(length_profile(count, total, most, slope), jnp.int32)
    twos = (count - 1) // 2
    source_of, sink = tallies[1:1 + 2 * twos:2], tallies[2:2 + 2 * twos:2]
    room = jnp.minimum(source_of - 1, most - sink)
    shifted = jax.random.randint(jax.random.fold_in(key, 1), (twos,), 0, 1 << 20) % (room + 1)
    tallies = tallies.at[1:1 + 2 * twos:2].set(source_of - shifted).at[2:2 + 2 * twos:2].set(sink + shifted)
    return tallies[jax.random.permutation(jax.random.fold_in(key, 2), count)]


def routed_block(stream_key, own, number, rows, number_of, top, limit, slope):
    ranking = jax.random.permutation(stream_key, number_of)
    packed, usual = shares(number_of, rows * top, limit, slope, True), shares(number_of, rows * top, limit, slope, False)
    places = jnp.arange(number_of)

    def named(sizes, turn):
        used = int((sizes > 0).sum())
        fixed = max(1, used // 4)
        passed = fixed + (places - fixed + turn * (used - fixed)) % max(1, number_of - fixed)
        return jnp.zeros((number_of,), jnp.int32).at[ranking[jnp.where(places < fixed, places, passed)]].set(jnp.asarray(sizes, jnp.int32))

    sizes = jnp.where(number % 4 == 0, named(packed, number // 4), named(usual, number - number // 4 - 1))
    mixed = jax.random.permutation(jax.random.fold_in(own, 3), number_of)
    giver, sink = mixed[0:number_of // 2 * 2:2], mixed[1:number_of // 2 * 2:2]
    room = jnp.minimum(sizes[giver] - 1, limit - sizes[sink]) // 2
    room = jnp.where((giver == ranking[0]) | (sink == ranking[0]) | (sizes[sink] == 0), 0, jnp.maximum(room, 0))
    passed = jax.random.randint(jax.random.fold_in(own, 4), (number_of // 2,), 0, 1 << 20) % (room + 1)
    sizes = sizes.at[giver].add(-passed).at[sink].add(passed)
    members = jnp.searchsorted(jnp.cumsum(sizes), jnp.arange(rows * top), side="right").astype(jnp.int32)
    listing = members.reshape(top, rows).T
    listing = listing[jax.random.permutation(jax.random.fold_in(own, 1), rows)]
    turn = jax.random.randint(jax.random.fold_in(own, 2), (rows, 1), 0, top)
    return jnp.take_along_axis(listing, (jnp.arange(top)[None, :] + turn) % top, axis=1)


def shares(count, total, bound, lean, full):
    weights = [(1 << 20) // math.isqrt(grade ** lean) + 1 for grade in range(1, count + 1)]
    largest = bound if full else min(bound, max(-(-total // count), total * weights[0] // sum(weights)))
    least = 1 if total - largest >= count - 1 else 0
    counts, spare = [largest] + [least] * (count - 1), total - largest - least * (count - 1)
    while spare > 0:
        candidates = [i for i in range(1, count) if counts[i] < largest] or [i for i in range(1, count) if counts[i] < bound]
        pool, left = sum([weights[i] for i in candidates]), spare
        for i in candidates:
            extra = min(bound - counts[i], max(1, left * weights[i] // pool), spare)
            counts[i] = counts[i] + extra
            spare = spare - extra
    return np.array(counts)


def scatter_about(stream_key, extent, scale, limit, split=(), kind=jnp.bfloat16):
    entries = scale * jax.random.normal(stream_key, extent, jnp.float32)
    if split:
        entries = entries * shard_levels(stream_key, extent, split, -0.22, 0.18)
    return jnp.clip(entries, -limit, limit).astype(kind)


def setup_inputs(seed: int = 0) -> dict:
    splits = jax.random.split(jax.random.key(seed), 13)
    states = scatter_about(splits[0], (2, TOKENS, D), 1.0, 6.0, ((1, 128),))
    lengths = jax.vmap(lambda own: ragged(own, SEQ_DEV, TOK_DEV, LEN_MAX, 2))(jax.random.split(splits[1], (N_REQ * N_EXP))).reshape((N_REQ * N_EXP, SEQ_DEV)).astype(jnp.int32)
    targets = plant(ranked_ids(splits[2], (TOKENS,), VOCAB, 2), jax.random.fold_in(splits[2], 3), 0, VOCAB - 1).astype(jnp.int32)
    routes_keys = jax.random.split(jax.random.fold_in(splits[3], 1), 2 * TOKENS // TOK_DEV)
    routes_turns = jax.random.permutation(jax.random.fold_in(splits[3], 3), 2 * TOKENS // TOK_DEV)
    routes = jax.vmap(lambda own, number: routed_block(jax.random.fold_in(splits[3], 2), own, number, TOK_DEV, EXPERTS, TOP, CAP, 1))(routes_keys, routes_turns).reshape((2, TOKENS, TOP))
    gate_probs = jnp.clip(jnp.exp(math.log(0.4) - 2.9957323 * jax.random.uniform(splits[4], (2, TOKENS, TOP), jnp.float32) ** shard_levels(splits[4], (2, TOKENS, TOP), ((1, 128),), -0.2, 0.2)), 0.02, 0.4)
    owners = jax.random.permutation(splits[5], SEQUENCES).astype(jnp.int32)
    norm_gains = jnp.clip(1.0 + 0.15 * jax.random.normal(splits[6], (2, 3, D), jnp.float32), 0.25, 1.75)
    qkv_weight = draw_qkv_weight(jax.random.fold_in(splits[12], 71), 0)
    out_weight = scatter_about(splits[8], (2, HEADS * HEAD_DIM, D), (HEADS * HEAD_DIM) ** -0.5, 0.1875)
    expert_in = scatter_about(splits[9], (2, EXPERTS, D, 2 * EXPERT_FF), D ** -0.5, 0.1875, ((1, 32),))
    expert_down = scatter_about(splits[10], (2, EXPERTS, EXPERT_FF, D), EXPERT_FF ** -0.5, 0.25, ((1, 32),))
    vocab_head = draw_vocab_head(jax.random.fold_in(splits[12], 71), 0)
    return dict(states=states, lengths=lengths, targets=targets, routes=routes, gate_probs=gate_probs, owners=owners, norm_gains=norm_gains, qkv_weight=qkv_weight, out_weight=out_weight, expert_in=expert_in, expert_down=expert_down, vocab_head=vocab_head)


EPSILON = 1e-06
RESIDUAL_SCALE = 0.22
SCORE_SCALE = 0.015625
LOGIT_DIVISOR = 6.0
ROTARY_BASE = 10000.0

def root_norm(values, gain_row):
    values = values.astype(jnp.float32)
    scaled = lax.rsqrt(lax.optimization_barrier(jnp.mean(values * values, axis=-1, keepdims=True)) + EPSILON)
    return values * scaled * gain_row

def segment_table(length_row, token_count):
    seq_ends = jnp.cumsum(length_row).astype(jnp.int32)
    seq_starts = (seq_ends - length_row).astype(jnp.int32)
    places = jnp.arange(token_count, dtype=jnp.int32)
    segment = lax.optimization_barrier(jnp.sum((places[:, None] >= seq_ends[None, :]).astype(jnp.int32), axis=1)).astype(jnp.int32)
    member = segment[:, None] == jnp.arange(length_row.shape[0], dtype=jnp.int32)[None, :]
    position = (places - lax.optimization_barrier(jnp.sum(member.astype(jnp.int32) * seq_starts[None, :], axis=1))).astype(jnp.int32)
    return (segment, member, position)

def rotary(values, position):
    half_dim = values.shape[-1] // 2
    frequency = ROTARY_BASE ** (-2.0 * jnp.arange(half_dim, dtype=jnp.float32) / values.shape[-1])
    angles = position.astype(jnp.float32)[:, None] * frequency[None, :]
    angles = jnp.concatenate([angles, angles], axis=-1)[:, None, :]
    leading = values[..., :half_dim]
    trailing = values[..., half_dim:]
    turned = jnp.concatenate([-trailing, leading], axis=-1)
    return values * jnp.cos(angles) + turned * jnp.sin(angles)

def attend(block_states, segment, position, gain_row, qkv_weight, out_weight):
    token_count = block_states.shape[0]
    group_size = HEADS // KV_HEADS
    normed = root_norm(block_states, gain_row).astype(jnp.bfloat16)
    mixed = jnp.dot(normed, qkv_weight, preferred_element_type=jnp.float32)
    queries = rotary(mixed[:, :HEADS * HEAD_DIM].reshape(token_count, HEADS, HEAD_DIM), position).astype(jnp.bfloat16)
    keys_all = rotary(mixed[:, HEADS * HEAD_DIM:(HEADS + KV_HEADS) * HEAD_DIM].reshape(token_count, KV_HEADS, HEAD_DIM), position).astype(jnp.bfloat16)
    values_all = mixed[:, (HEADS + KV_HEADS) * HEAD_DIM:].reshape(token_count, KV_HEADS, HEAD_DIM).astype(jnp.bfloat16)
    grouped = queries.reshape(token_count, KV_HEADS, group_size, HEAD_DIM)
    scores = jnp.einsum('tgqd,sgd->gqts', grouped.astype(jnp.float32), keys_all.astype(jnp.float32)) * SCORE_SCALE
    places = jnp.arange(token_count, dtype=jnp.int32)
    allowed = (segment[:, None] == segment[None, :]) & (places[None, :] <= places[:, None])
    scores = jnp.where(allowed, scores, -1e+30)
    highest = lax.optimization_barrier(jnp.max(scores, axis=-1, keepdims=True))
    weights = jnp.exp(scores - highest)
    weights = (weights / lax.optimization_barrier(jnp.sum(weights, axis=-1, keepdims=True))).astype(jnp.bfloat16)
    attended = jnp.einsum('gqts,sgd->tgqd', weights.astype(jnp.float32), values_all.astype(jnp.float32)).astype(jnp.bfloat16)
    projected = jnp.dot(attended.reshape(token_count, HEADS * HEAD_DIM), out_weight, preferred_element_type=jnp.float32)
    return (block_states.astype(jnp.float32) + RESIDUAL_SCALE * projected).astype(jnp.bfloat16)

def reference(states, lengths, targets, routes, gate_probs, owners, norm_gains, qkv_weight, out_weight, expert_in, expert_down, vocab_head):
    devices = N_REQ * N_EXP
    token_count = TOK_DEV

    def attention_block(operands):
        block_states, length_row = operands
        segment, member, position = segment_table(length_row, token_count)
        return jnp.stack([attend(block_states[which], segment, position, norm_gains[which, 0], qkv_weight[which], out_weight[which]) for which in range(2)])
    blocks = jnp.transpose(states.reshape(2, devices, token_count, D), (1, 0, 2, 3))
    residual = lax.map(attention_block, (blocks, lengths))
    residual = jnp.transpose(residual, (1, 0, 2, 3)).reshape(2, devices * token_count, D)
    moe_in = root_norm(residual, norm_gains[:, 1][:, None, :]).astype(jnp.bfloat16)
    flat_routes = routes.reshape(2, devices, token_count * TOP)
    onehot = (flat_routes[..., None] == jnp.arange(EXPERTS, dtype=jnp.int32)).astype(jnp.int32)
    rank_slot = lax.optimization_barrier(jnp.sum((jnp.cumsum(onehot, axis=2).astype(jnp.int32) - 1) * onehot, axis=3)).astype(jnp.int32)
    device_index = jnp.arange(devices, dtype=jnp.int32)[None, :, None]
    slot_index = (flat_routes * (devices * CAP) + device_index * CAP + rank_slot).reshape(2, -1)
    token_index = device_index * token_count + jnp.arange(token_count * TOP, dtype=jnp.int32)[None, None, :] // TOP
    token_index = jnp.broadcast_to(token_index, flat_routes.shape).reshape(2, -1)
    mixtures = []
    for which in range(2):
        row_index = jnp.zeros((EXPERTS * devices * CAP,), jnp.int32).at[slot_index[which]].set(token_index[which]).reshape(EXPERTS, devices * CAP)
        weight = jnp.zeros((EXPERTS * devices * CAP,), jnp.float32).at[slot_index[which]].set(gate_probs[which].reshape(-1)).reshape(EXPERTS, devices * CAP)
        source = moe_in[which]

        def expert_step(totals, operands):
            picked, gate_weight, first_matrix, second_matrix = operands
            inputs = source[picked]
            gate_up = jnp.dot(inputs, first_matrix, preferred_element_type=jnp.float32)
            hidden = (jax.nn.silu(gate_up[:, :EXPERT_FF]) * gate_up[:, EXPERT_FF:]).astype(jnp.bfloat16)
            produced = jnp.dot(hidden, second_matrix, preferred_element_type=jnp.float32).astype(jnp.bfloat16)
            return (totals.at[picked].add(gate_weight[:, None] * produced.astype(jnp.float32)), None)
        totals, unused = lax.scan(expert_step, jnp.zeros((devices * token_count, D), jnp.float32), (row_index, weight, expert_in[which], expert_down[which]))
        mixtures.append(totals)
    mixture = jnp.stack(mixtures)
    final = root_norm(residual.astype(jnp.float32) + RESIDUAL_SCALE * mixture, norm_gains[:, 2][:, None, :]).astype(jnp.bfloat16)

    def head_block(operands):
        row_block, wanted = operands
        results = []
        for which in range(2):
            logits = jnp.dot(row_block[which], vocab_head[which].T, preferred_element_type=jnp.float32) / LOGIT_DIVISOR
            highest = lax.optimization_barrier(jnp.max(logits, axis=1, keepdims=True))
            log_total = highest[:, 0] + jnp.log(lax.optimization_barrier(jnp.sum(jnp.exp(logits - highest), axis=1)))
            chosen = jnp.take_along_axis(logits, wanted[:, None], axis=1)[:, 0]
            results.append(chosen - log_total)
        return jnp.stack(results)
    final_blocks = jnp.transpose(final.reshape(2, devices, token_count, D), (1, 0, 2, 3))
    token_logp = lax.map(head_block, (final_blocks, targets.reshape(devices, token_count)))
    token_logp = jnp.transpose(token_logp, (1, 0, 2)).reshape(2, devices * token_count)
    difference = (token_logp[0] - token_logp[1]).reshape(devices, token_count)

    def sequence_sums(length_row, values):
        segment, member, position = segment_table(length_row, token_count)
        return lax.optimization_barrier(jnp.sum(member.astype(jnp.float32) * values[:, None], axis=0))
    seq_sums = jax.vmap(sequence_sums)(lengths, difference)
    seq_totals = jnp.zeros((devices * SEQ_DEV,), jnp.float32).at[owners].set(seq_sums.reshape(-1))
    return (token_logp, seq_totals)
```

```python
import jax
import jax.numpy as jnp
from jax import lax
from jax.sharding import PartitionSpec as P

HEADS = 16
KV_HEADS = 8
HEAD_DIM = 64
EXPERT_FF = 512
EXPERTS = 32
TOP = 8
CAP = 40


EPSILON = 1e-06
RESIDUAL_SCALE = 0.22
SCORE_SCALE = 0.015625
LOGIT_DIVISOR = 6.0
ROTARY_BASE = 10000.0


def combined_all(x, axis, combine):
    everything = jax.tree.map(lambda part: lax.all_gather(part, axis), x)
    initial = jax.tree.map(lambda part: part[0], everything)

    def step(k, so_far):
        return combine(so_far, jax.tree.map(lambda part: part[k], everything))

    return lax.fori_loop(1, lax.axis_size(axis), step, initial)


def root_norm(values, gain_row):
    values = values.astype(jnp.float32)
    scaled = lax.rsqrt(jnp.mean(values * values, axis=-1, keepdims=True) + EPSILON)
    return values * scaled * gain_row


def segment_table(length_row, token_count):
    seq_ends = jnp.cumsum(length_row)
    seq_starts = seq_ends - length_row
    places = jnp.arange(token_count, dtype=jnp.int32)
    segment = jnp.sum((places[:, None] >= seq_ends[None, :]).astype(jnp.int32), axis=1)
    member = segment[:, None] == jnp.arange(length_row.shape[0], dtype=jnp.int32)[None, :]
    position = places - jnp.sum(member.astype(jnp.int32) * seq_starts[None, :], axis=1)
    return (segment, member, position)


def rotary(values, position):
    half_dim = values.shape[-1] // 2
    frequency = ROTARY_BASE ** (-2.0 * jnp.arange(half_dim, dtype=jnp.float32) / values.shape[-1])
    angles = position.astype(jnp.float32)[:, None] * frequency[None, :]
    angles = jnp.concatenate([angles, angles], axis=-1)[:, None, :]
    leading = values[..., :half_dim]
    trailing = values[..., half_dim:]
    turned = jnp.concatenate([-trailing, leading], axis=-1)
    return values * jnp.cos(angles) + turned * jnp.sin(angles)


def attend(block_states, segment, position, gain_row, qkv_weight, out_weight):
    token_count = block_states.shape[0]
    group_size = HEADS // KV_HEADS
    normed = root_norm(block_states, gain_row).astype(jnp.bfloat16)
    mixed = jnp.dot(normed, qkv_weight, preferred_element_type=jnp.float32)
    queries = rotary(
        mixed[:, : HEADS * HEAD_DIM].reshape(token_count, HEADS, HEAD_DIM), position
    ).astype(jnp.bfloat16)
    keys_all = rotary(
        mixed[:, HEADS * HEAD_DIM : (HEADS + KV_HEADS) * HEAD_DIM].reshape(
            token_count, KV_HEADS, HEAD_DIM
        ),
        position,
    ).astype(jnp.bfloat16)
    values_all = (
        mixed[:, (HEADS + KV_HEADS) * HEAD_DIM :]
        .reshape(token_count, KV_HEADS, HEAD_DIM)
        .astype(jnp.bfloat16)
    )
    grouped = queries.reshape(token_count, KV_HEADS, group_size, HEAD_DIM)
    scores = (
        jnp.einsum("tgqd,sgd->gqts", grouped, keys_all, preferred_element_type=jnp.float32)
        * SCORE_SCALE
    )
    places = jnp.arange(token_count, dtype=jnp.int32)
    allowed = (segment[:, None] == segment[None, :]) & (places[None, :] <= places[:, None])
    scores = jnp.where(allowed, scores, -1e30)
    highest = jnp.max(scores, axis=-1, keepdims=True)
    weights = jnp.exp(scores - highest)
    weights = (weights / jnp.sum(weights, axis=-1, keepdims=True)).astype(jnp.bfloat16)
    attended = jnp.einsum(
        "gqts,sgd->tgqd", weights, values_all, preferred_element_type=jnp.float32
    ).astype(jnp.bfloat16)
    projected = jnp.dot(
        attended.reshape(token_count, HEADS * HEAD_DIM),
        out_weight,
        preferred_element_type=jnp.float32,
    )
    return (block_states.astype(jnp.float32) + RESIDUAL_SCALE * projected).astype(jnp.bfloat16)


def join_parts(first_part, second_part):
    first_max, first_mass, first_hit = first_part
    second_max, second_mass, second_hit = second_part
    joined_max = jnp.maximum(first_max, second_max)
    joined_mass = first_mass * jnp.exp(first_max - joined_max) + second_mass * jnp.exp(
        second_max - joined_max
    )
    return (joined_max, joined_mass, first_hit + second_hit)


def per_device(
    states,
    lengths,
    targets,
    routes,
    gate_probs,
    owners,
    norm_gains,
    qkv_weight,
    out_weight,
    expert_in,
    expert_down,
    vocab_head,
):
    token_count = states.shape[1]
    width = states.shape[2]
    segment, member, position = segment_table(lengths[0], token_count)
    residual = jnp.stack(
        [
            attend(
                states[which],
                segment,
                position,
                norm_gains[which, 0],
                qkv_weight[which],
                out_weight[which],
            )
            for which in range(2)
        ]
    )
    moe_in = root_norm(residual, norm_gains[:, 1][:, None, :]).astype(jnp.bfloat16)
    groups = lax.axis_size("exp")
    local_count = expert_in.shape[1]
    flat_routes = routes.reshape(2, token_count * TOP)
    onehot = (flat_routes[..., None] == jnp.arange(EXPERTS, dtype=jnp.int32)).astype(jnp.int32)
    rank_slot = jnp.sum((jnp.cumsum(onehot, axis=1) - 1) * onehot, axis=2)
    slot_index = (
        flat_routes * CAP + rank_slot + jnp.arange(2, dtype=jnp.int32)[:, None] * (EXPERTS * CAP)
    ).reshape(-1)
    token_index = jnp.arange(token_count * TOP, dtype=jnp.int32) // TOP
    outgoing = (
        jnp.zeros((2 * EXPERTS * CAP, width), jnp.bfloat16)
        .at[slot_index]
        .set(moe_in[:, token_index].reshape(-1, width))
    )
    arrived = lax.all_to_all(
        outgoing.reshape(2, groups, local_count * CAP, width),
        "exp",
        split_axis=1,
        concat_axis=1,
        tiled=True,
    )
    inputs = arrived.reshape(2, groups, local_count, CAP, width)
    gate_up = jnp.einsum("mslcd,mldf->mslcf", inputs, expert_in, preferred_element_type=jnp.float32)
    hidden = (jax.nn.silu(gate_up[..., :EXPERT_FF]) * gate_up[..., EXPERT_FF:]).astype(jnp.bfloat16)
    produced = jnp.einsum(
        "mslcf,mlfd->mslcd", hidden, expert_down, preferred_element_type=jnp.float32
    ).astype(jnp.bfloat16)
    returned = lax.all_to_all(
        produced.reshape(2, groups, local_count * CAP, width),
        "exp",
        split_axis=1,
        concat_axis=1,
        tiled=True,
    )
    picked = returned.reshape(2 * EXPERTS * CAP, width)[slot_index].reshape(
        2, token_count, TOP, width
    )
    mixture = jnp.sum(gate_probs[..., None] * picked.astype(jnp.float32), axis=2)
    final = root_norm(
        residual.astype(jnp.float32) + RESIDUAL_SCALE * mixture, norm_gains[:, 2][:, None, :]
    ).astype(jnp.bfloat16)
    shard = lax.axis_index("exp")
    vocab_rows = vocab_head.shape[1]
    lowest = shard * vocab_rows
    vocab_ids = jnp.arange(vocab_rows, dtype=jnp.int32)
    shard_piece = lax.all_gather(final, "exp", axis=1, tiled=True)
    piece_rows = shard_piece.shape[1]
    block_rows = 512
    block_count = piece_rows // block_rows
    wanted_all = targets - lowest

    def one_block(block_number):
        row_block = lax.dynamic_slice_in_dim(shard_piece, block_number * block_rows, block_rows, 1)
        wanted = lax.dynamic_slice_in_dim(wanted_all, block_number * block_rows, block_rows, 0)
        logits = (
            jnp.einsum("mtd,mvd->mtv", row_block, vocab_head, preferred_element_type=jnp.float32)
            / LOGIT_DIVISOR
        )
        highest = jnp.max(logits, axis=2)
        masses = jnp.sum(jnp.exp(logits - highest[..., None]), axis=2)
        chosen = jnp.sum(
            jnp.where(wanted[None, :, None] == vocab_ids[None, None, :], logits, 0.0), axis=2
        )
        return (highest, masses, chosen)

    block_max, block_mass, block_hit = lax.map(one_block, jnp.arange(block_count, dtype=jnp.int32))

    def place(fresh):
        ordered = jnp.transpose(fresh, (1, 0, 2)).reshape(2, piece_rows)
        return ordered

    groups_exp = lax.axis_size("exp")
    stacked = jnp.stack([place(block_max), place(block_mass), place(block_hit)])
    stacked = jnp.transpose(stacked.reshape(3, 2, groups_exp, token_count), (2, 0, 1, 3))
    gathered = lax.all_to_all(stacked, "exp", 0, 0, tiled=True)
    all_max = gathered[:, 0]
    all_mass = gathered[:, 1]
    all_hit = gathered[:, 2]
    final_max = jnp.max(all_max, axis=0)
    final_mass = jnp.sum(all_mass * jnp.exp(all_max - final_max[None]), axis=0)
    final_hit = jnp.sum(all_hit, axis=0)
    token_logp = final_hit - (final_max + jnp.log(final_mass))
    difference = token_logp[0] - token_logp[1]
    seq_sums = jnp.sum(member.astype(jnp.float32) * difference[:, None], axis=0)
    devices = lax.axis_size("req") * lax.axis_size("exp")
    per_device_seqs = seq_sums.shape[0]
    everyone = devices * per_device_seqs
    dense_totals = jnp.sum(
        (owners[:, None] == jnp.arange(everyone, dtype=jnp.int32)[None, :]).astype(jnp.float32)
        * seq_sums[:, None],
        axis=0,
    )
    delivered = lax.all_to_all(
        dense_totals.reshape(devices, per_device_seqs), ("req", "exp"), 0, 0, tiled=True
    )
    seq_totals = jnp.sum(delivered, axis=0)
    return (token_logp, seq_totals)


def solution(mesh):
    in_specs = (
        P(None, ("req", "exp"), None),
        P(("req", "exp"), None),
        P("req"),
        P(None, ("req", "exp"), None),
        P(None, ("req", "exp"), None),
        P(("req", "exp")),
        P(),
        P(),
        P(),
        P(None, "exp", None, None),
        P(None, "exp", None, None),
        P(None, "exp", None),
    )
    out_specs = (P(None, ("req", "exp")), P(("req", "exp")))
    return jax.shard_map(
        per_device, mesh=mesh, in_specs=in_specs, out_specs=out_specs, check_vma=False
    )
```

```python
import jax
import jax.numpy as jnp
from jax import lax
from jax.sharding import PartitionSpec as P

HEADS = 16
KV_HEADS = 8
HEAD_DIM = 64
EXPERT_FF = 512
EXPERTS = 32
TOP = 8
CAP = 40


EPSILON = 1e-06
RESIDUAL_SCALE = 0.22
SCORE_SCALE = 0.015625
LOGIT_DIVISOR = 6.0
ROTARY_BASE = 10000.0


def combined_all(x, axis, combine):
    everything = jax.tree.map(lambda part: lax.all_gather(part, axis), x)
    initial = jax.tree.map(lambda part: part[0], everything)

    def step(k, so_far):
        return combine(so_far, jax.tree.map(lambda part: part[k], everything))

    return lax.fori_loop(1, lax.axis_size(axis), step, initial)


def root_norm(values, gain_row):
    values = values.astype(jnp.float32)
    scaled = lax.rsqrt(jnp.mean(values * values, axis=-1, keepdims=True) + EPSILON)
    return values * scaled * gain_row


def segment_table(length_row, token_count):
    seq_ends = jnp.cumsum(length_row)
    seq_starts = seq_ends - length_row
    places = jnp.arange(token_count, dtype=jnp.int32)
    segment = jnp.sum((places[:, None] >= seq_ends[None, :]).astype(jnp.int32), axis=1)
    member = segment[:, None] == jnp.arange(length_row.shape[0], dtype=jnp.int32)[None, :]
    position = places - jnp.sum(member.astype(jnp.int32) * seq_starts[None, :], axis=1)
    return (segment, member, position)


def rotary(values, position):
    half_dim = values.shape[-1] // 2
    frequency = ROTARY_BASE ** (-2.0 * jnp.arange(half_dim, dtype=jnp.float32) / values.shape[-1])
    angles = position.astype(jnp.float32)[:, None] * frequency[None, :]
    angles = jnp.concatenate([angles, angles], axis=-1)[:, None, :]
    leading = values[..., :half_dim]
    trailing = values[..., half_dim:]
    turned = jnp.concatenate([-trailing, leading], axis=-1)
    return values * jnp.cos(angles) + turned * jnp.sin(angles)


def attend(block_states, segment, position, gain_row, qkv_weight, out_weight):
    token_count = block_states.shape[0]
    group_size = HEADS // KV_HEADS
    normed = root_norm(block_states, gain_row).astype(jnp.bfloat16)
    mixed = jnp.dot(normed, qkv_weight, preferred_element_type=jnp.float32)
    queries = rotary(
        mixed[:, : HEADS * HEAD_DIM].reshape(token_count, HEADS, HEAD_DIM), position
    ).astype(jnp.bfloat16)
    keys_all = rotary(
        mixed[:, HEADS * HEAD_DIM : (HEADS + KV_HEADS) * HEAD_DIM].reshape(
            token_count, KV_HEADS, HEAD_DIM
        ),
        position,
    ).astype(jnp.bfloat16)
    values_all = (
        mixed[:, (HEADS + KV_HEADS) * HEAD_DIM :]
        .reshape(token_count, KV_HEADS, HEAD_DIM)
        .astype(jnp.bfloat16)
    )
    grouped = queries.reshape(token_count, KV_HEADS, group_size, HEAD_DIM)
    scores = (
        jnp.einsum("tgqd,sgd->gqts", grouped, keys_all, preferred_element_type=jnp.float32)
        * SCORE_SCALE
    )
    places = jnp.arange(token_count, dtype=jnp.int32)
    allowed = (segment[:, None] == segment[None, :]) & (places[None, :] <= places[:, None])
    scores = jnp.where(allowed, scores, -1e30)
    highest = jnp.max(scores, axis=-1, keepdims=True)
    weights = jnp.exp(scores - highest)
    weights = (weights / jnp.sum(weights, axis=-1, keepdims=True)).astype(jnp.bfloat16)
    attended = jnp.einsum(
        "gqts,sgd->tgqd", weights, values_all, preferred_element_type=jnp.float32
    ).astype(jnp.bfloat16)
    projected = jnp.dot(
        attended.reshape(token_count, HEADS * HEAD_DIM),
        out_weight,
        preferred_element_type=jnp.float32,
    )
    return (block_states.astype(jnp.float32) + RESIDUAL_SCALE * projected).astype(jnp.bfloat16)


def join_parts(first_part, second_part):
    first_max, first_mass, first_hit = first_part
    second_max, second_mass, second_hit = second_part
    joined_max = jnp.maximum(first_max, second_max)
    joined_mass = first_mass * jnp.exp(first_max - joined_max) + second_mass * jnp.exp(
        second_max - joined_max
    )
    return (joined_max, joined_mass, first_hit + second_hit)


def per_device(
    states,
    lengths,
    targets,
    routes,
    gate_probs,
    owners,
    norm_gains,
    qkv_weight,
    out_weight,
    expert_in,
    expert_down,
    vocab_head,
):
    token_count = states.shape[1]
    width = states.shape[2]
    segment, member, position = segment_table(lengths[0], token_count)
    residual = jnp.stack(
        [
            attend(
                states[which],
                segment,
                position,
                norm_gains[which, 0],
                qkv_weight[which],
                out_weight[which],
            )
            for which in range(2)
        ]
    )
    moe_in = root_norm(residual, norm_gains[:, 1][:, None, :]).astype(jnp.bfloat16)
    groups = lax.axis_size("exp")
    local_count = expert_in.shape[1]
    flat_routes = routes.reshape(2, token_count * TOP)
    pairs = token_count * TOP
    slots = EXPERTS * CAP
    onehot = (flat_routes[..., None] == jnp.arange(EXPERTS, dtype=jnp.int32)).astype(jnp.bfloat16)
    pair_ids = jnp.arange(pairs, dtype=jnp.int32)
    lower = (pair_ids[None, :] <= pair_ids[:, None]).astype(jnp.bfloat16)
    running = jnp.einsum("ij,mje->mie", lower, onehot, preferred_element_type=jnp.float32)
    rank_slot = jnp.sum((running - 1.0) * onehot.astype(jnp.float32), axis=2).astype(jnp.int32)
    local_slot = (flat_routes * CAP + rank_slot).reshape(2, token_count, TOP)
    slot_ids = jnp.arange(slots, dtype=jnp.int32)
    chooser = jnp.sum(
        (local_slot[:, None, :, :] == slot_ids[None, :, None, None]).astype(jnp.bfloat16),
        axis=3,
        dtype=jnp.bfloat16,
    )
    outgoing = jnp.einsum(
        "mst,mtd->msd", chooser, moe_in, preferred_element_type=jnp.float32
    ).astype(jnp.bfloat16)
    arrived = lax.all_to_all(
        outgoing.reshape(2, groups, local_count * CAP, width),
        "exp",
        split_axis=1,
        concat_axis=1,
        tiled=True,
    )
    inputs = arrived.reshape(2, groups, local_count, CAP, width)
    gate_up = jnp.einsum("mslcd,mldf->mslcf", inputs, expert_in, preferred_element_type=jnp.float32)
    hidden = (jax.nn.silu(gate_up[..., :EXPERT_FF]) * gate_up[..., EXPERT_FF:]).astype(jnp.bfloat16)
    produced = jnp.einsum(
        "mslcf,mlfd->mslcd", hidden, expert_down, preferred_element_type=jnp.float32
    ).astype(jnp.bfloat16)
    returned = lax.all_to_all(
        produced.reshape(2, groups, local_count * CAP, width),
        "exp",
        split_axis=1,
        concat_axis=1,
        tiled=True,
    ).reshape(2, slots, width)
    picker = (local_slot[..., None] == slot_ids[None, None, None, :]).astype(jnp.bfloat16)
    picked = jnp.einsum("mtks,msd->mtkd", picker, returned, preferred_element_type=jnp.float32)
    mixture = jnp.sum(gate_probs[..., None] * picked, axis=2)
    final = root_norm(
        residual.astype(jnp.float32) + RESIDUAL_SCALE * mixture, norm_gains[:, 2][:, None, :]
    ).astype(jnp.bfloat16)
    shard = lax.axis_index("exp")
    vocab_rows = vocab_head.shape[1]
    lowest = shard * vocab_rows
    vocab_ids = jnp.arange(vocab_rows, dtype=jnp.int32)
    groups_exp = lax.axis_size("exp")
    halves = 2
    half_rows = token_count // halves
    wanted_all = (targets - lowest).reshape(groups_exp, halves, half_rows)
    block_rows = 512
    pieces = []
    for which in range(2):
        for half in range(halves):
            chunk = lax.all_gather(
                final[which, half * half_rows : (half + 1) * half_rows], "exp", axis=0, tiled=True
            )
            chunk_rows = chunk.shape[0]
            block_count = chunk_rows // block_rows
            wanted_chunk = wanted_all[:, half].reshape(chunk_rows)
            head = vocab_head[which]

            def one_block(block_number, chunk=chunk, wanted_chunk=wanted_chunk, head=head):
                row_block = lax.dynamic_slice_in_dim(chunk, block_number * block_rows, block_rows, 0)
                wanted = lax.dynamic_slice_in_dim(wanted_chunk, block_number * block_rows, block_rows, 0)
                logits = (
                    jnp.einsum("td,vd->tv", row_block, head, preferred_element_type=jnp.float32)
                    / LOGIT_DIVISOR
                )
                highest = jnp.max(logits, axis=1)
                masses = jnp.sum(jnp.exp(logits - highest[:, None]), axis=1)
                chosen = jnp.sum(
                    jnp.where(wanted[:, None] == vocab_ids[None, :], logits, 0.0), axis=1
                )
                return jnp.stack([highest, masses, chosen])

            stats = lax.map(one_block, jnp.arange(block_count, dtype=jnp.int32))
            stats = jnp.transpose(stats, (1, 0, 2)).reshape(3, groups_exp, half_rows)
            pieces.append(stats)
    stacked = jnp.stack(
        [jnp.concatenate([pieces[which * halves + half] for half in range(halves)], axis=2) for which in range(2)]
    )
    stacked = jnp.transpose(stacked, (2, 1, 0, 3))
    gathered = lax.all_to_all(stacked, "exp", 0, 0, tiled=True)
    all_max = gathered[:, 0]
    all_mass = gathered[:, 1]
    all_hit = gathered[:, 2]
    final_max = jnp.max(all_max, axis=0)
    final_mass = jnp.sum(all_mass * jnp.exp(all_max - final_max[None]), axis=0)
    final_hit = jnp.sum(all_hit, axis=0)
    token_logp = final_hit - (final_max + jnp.log(final_mass))
    difference = token_logp[0] - token_logp[1]
    seq_sums = jnp.sum(member.astype(jnp.float32) * difference[:, None], axis=0)
    devices = lax.axis_size("req") * lax.axis_size("exp")
    per_device_seqs = seq_sums.shape[0]
    everyone = devices * per_device_seqs
    dense_totals = jnp.sum(
        (owners[:, None] == jnp.arange(everyone, dtype=jnp.int32)[None, :]).astype(jnp.float32)
        * seq_sums[:, None],
        axis=0,
    )
    delivered = lax.all_to_all(
        dense_totals.reshape(devices, per_device_seqs), ("req", "exp"), 0, 0, tiled=True
    )
    seq_totals = jnp.sum(delivered, axis=0)
    return (token_logp, seq_totals)


def solution(mesh):
    in_specs = (
        P(None, ("req", "exp"), None),
        P(("req", "exp"), None),
        P("req"),
        P(None, ("req", "exp"), None),
        P(None, ("req", "exp"), None),
        P(("req", "exp")),
        P(),
        P(),
        P(),
        P(None, "exp", None, None),
        P(None, "exp", None, None),
        P(None, "exp", None),
    )
    out_specs = (P(None, ("req", "exp")), P(("req", "exp")))
    return jax.shard_map(
        per_device, mesh=mesh, in_specs=in_specs, out_specs=out_specs, check_vma=False
    )
```

```python
import jax
import jax.numpy as jnp
from jax import lax
from jax.sharding import PartitionSpec as P

HEADS = 16
KV_HEADS = 8
HEAD_DIM = 64
EXPERT_FF = 512
EXPERTS = 32
TOP = 8
CAP = 40


EPSILON = 1e-06
RESIDUAL_SCALE = 0.22
SCORE_SCALE = 0.015625
LOGIT_DIVISOR = 6.0
ROTARY_BASE = 10000.0


def combined_all(x, axis, combine):
    everything = jax.tree.map(lambda part: lax.all_gather(part, axis), x)
    initial = jax.tree.map(lambda part: part[0], everything)

    def step(k, so_far):
        return combine(so_far, jax.tree.map(lambda part: part[k], everything))

    return lax.fori_loop(1, lax.axis_size(axis), step, initial)


def root_norm(values, gain_row):
    values = values.astype(jnp.float32)
    scaled = lax.rsqrt(jnp.mean(values * values, axis=-1, keepdims=True) + EPSILON)
    return values * scaled * gain_row


def segment_table(length_row, token_count):
    seq_ends = jnp.cumsum(length_row)
    seq_starts = seq_ends - length_row
    places = jnp.arange(token_count, dtype=jnp.int32)
    segment = jnp.sum((places[:, None] >= seq_ends[None, :]).astype(jnp.int32), axis=1)
    member = segment[:, None] == jnp.arange(length_row.shape[0], dtype=jnp.int32)[None, :]
    position = places - jnp.sum(member.astype(jnp.int32) * seq_starts[None, :], axis=1)
    return (segment, member, position)


def rotary(values, position):
    half_dim = values.shape[-1] // 2
    frequency = ROTARY_BASE ** (-2.0 * jnp.arange(half_dim, dtype=jnp.float32) / values.shape[-1])
    angles = position.astype(jnp.float32)[:, None] * frequency[None, :]
    angles = jnp.concatenate([angles, angles], axis=-1)[:, None, :]
    leading = values[..., :half_dim]
    trailing = values[..., half_dim:]
    turned = jnp.concatenate([-trailing, leading], axis=-1)
    return values * jnp.cos(angles) + turned * jnp.sin(angles)


def attend(block_states, segment, position, gain_row, qkv_weight, out_weight):
    token_count = block_states.shape[0]
    group_size = HEADS // KV_HEADS
    normed = root_norm(block_states, gain_row).astype(jnp.bfloat16)
    mixed = jnp.dot(normed, qkv_weight, preferred_element_type=jnp.float32)
    queries = rotary(
        mixed[:, : HEADS * HEAD_DIM].reshape(token_count, HEADS, HEAD_DIM), position
    ).astype(jnp.bfloat16)
    keys_all = rotary(
        mixed[:, HEADS * HEAD_DIM : (HEADS + KV_HEADS) * HEAD_DIM].reshape(
            token_count, KV_HEADS, HEAD_DIM
        ),
        position,
    ).astype(jnp.bfloat16)
    values_all = (
        mixed[:, (HEADS + KV_HEADS) * HEAD_DIM :]
        .reshape(token_count, KV_HEADS, HEAD_DIM)
        .astype(jnp.bfloat16)
    )
    grouped = queries.reshape(token_count, KV_HEADS, group_size, HEAD_DIM)
    scores = (
        jnp.einsum("tgqd,sgd->gqts", grouped, keys_all, preferred_element_type=jnp.float32)
        * SCORE_SCALE
    )
    places = jnp.arange(token_count, dtype=jnp.int32)
    allowed = (segment[:, None] == segment[None, :]) & (places[None, :] <= places[:, None])
    scores = jnp.where(allowed, scores, -1e30)
    highest = jnp.max(scores, axis=-1, keepdims=True)
    weights = jnp.exp(scores - highest)
    weights = (weights / jnp.sum(weights, axis=-1, keepdims=True)).astype(jnp.bfloat16)
    attended = jnp.einsum(
        "gqts,sgd->tgqd", weights, values_all, preferred_element_type=jnp.float32
    ).astype(jnp.bfloat16)
    projected = jnp.dot(
        attended.reshape(token_count, HEADS * HEAD_DIM),
        out_weight,
        preferred_element_type=jnp.float32,
    )
    return (block_states.astype(jnp.float32) + RESIDUAL_SCALE * projected).astype(jnp.bfloat16)


def join_parts(first_part, second_part):
    first_max, first_mass, first_hit = first_part
    second_max, second_mass, second_hit = second_part
    joined_max = jnp.maximum(first_max, second_max)
    joined_mass = first_mass * jnp.exp(first_max - joined_max) + second_mass * jnp.exp(
        second_max - joined_max
    )
    return (joined_max, joined_mass, first_hit + second_hit)


def per_device(
    states,
    lengths,
    targets,
    routes,
    gate_probs,
    owners,
    norm_gains,
    qkv_weight,
    out_weight,
    expert_in,
    expert_down,
    vocab_head,
):
    token_count = states.shape[1]
    width = states.shape[2]
    segment, member, position = segment_table(lengths[0], token_count)
    groups = lax.axis_size("exp")
    local_count = expert_in.shape[1]
    pairs = token_count * TOP
    slots = EXPERTS * CAP
    pair_ids = jnp.arange(pairs, dtype=jnp.int32)
    lower = (pair_ids[None, :] <= pair_ids[:, None]).astype(jnp.bfloat16)
    slot_ids = jnp.arange(slots, dtype=jnp.int32)
    shard = lax.axis_index("exp")
    vocab_rows = vocab_head.shape[1]
    lowest = shard * vocab_rows
    vocab_ids = jnp.arange(vocab_rows, dtype=jnp.int32)
    wanted_all = targets - lowest
    block_rows = 512

    def model_final(which):
        residual = attend(
            states[which],
            segment,
            position,
            norm_gains[which, 0],
            qkv_weight[which],
            out_weight[which],
        )
        moe_in = root_norm(residual, norm_gains[which, 1]).astype(jnp.bfloat16)
        flat_routes = routes[which].reshape(pairs)
        onehot = (flat_routes[:, None] == jnp.arange(EXPERTS, dtype=jnp.int32)).astype(
            jnp.bfloat16
        )
        running = jnp.dot(lower, onehot, preferred_element_type=jnp.float32)
        rank_slot = jnp.sum((running - 1.0) * onehot.astype(jnp.float32), axis=1).astype(jnp.int32)
        local_slot = (flat_routes * CAP + rank_slot).reshape(token_count, TOP)
        chooser = jnp.sum(
            (local_slot[None, :, :] == slot_ids[:, None, None]).astype(jnp.bfloat16),
            axis=2,
            dtype=jnp.bfloat16,
        )
        outgoing = jnp.dot(chooser, moe_in, preferred_element_type=jnp.float32).astype(
            jnp.bfloat16
        )
        arrived = lax.all_to_all(
            outgoing.reshape(groups, local_count * CAP, width),
            "exp",
            split_axis=0,
            concat_axis=0,
            tiled=True,
        )
        inputs = arrived.reshape(groups, local_count, CAP, width)
        gate_up = jnp.einsum(
            "slcd,ldf->slcf", inputs, expert_in[which], preferred_element_type=jnp.float32
        )
        hidden = (jax.nn.silu(gate_up[..., :EXPERT_FF]) * gate_up[..., EXPERT_FF:]).astype(
            jnp.bfloat16
        )
        produced = jnp.einsum(
            "slcf,lfd->slcd", hidden, expert_down[which], preferred_element_type=jnp.float32
        ).astype(jnp.bfloat16)
        returned = lax.all_to_all(
            produced.reshape(groups, local_count * CAP, width),
            "exp",
            split_axis=0,
            concat_axis=0,
            tiled=True,
        ).reshape(slots, width)
        picker = (local_slot[..., None] == slot_ids[None, None, :]).astype(jnp.bfloat16)
        picked = jnp.einsum("tks,sd->tkd", picker, returned, preferred_element_type=jnp.float32)
        mixture = jnp.sum(gate_probs[which][..., None] * picked, axis=1)
        final = root_norm(
            residual.astype(jnp.float32) + RESIDUAL_SCALE * mixture, norm_gains[which, 2]
        ).astype(jnp.bfloat16)
        return final

    def model_stats(which, chunk):
        chunk_rows = chunk.shape[0]
        block_count = chunk_rows // block_rows
        head = vocab_head[which]

        def one_block(block_number):
            row_block = lax.dynamic_slice_in_dim(chunk, block_number * block_rows, block_rows, 0)
            wanted = lax.dynamic_slice_in_dim(wanted_all, block_number * block_rows, block_rows, 0)
            logits = (
                jnp.einsum("td,vd->tv", row_block, head, preferred_element_type=jnp.float32)
                / LOGIT_DIVISOR
            )
            highest = jnp.max(logits, axis=1)
            masses = jnp.sum(jnp.exp(logits - highest[:, None]), axis=1)
            chosen = jnp.sum(jnp.where(wanted[:, None] == vocab_ids[None, :], logits, 0.0), axis=1)
            return jnp.stack([highest, masses, chosen])

        stats = lax.map(one_block, jnp.arange(block_count, dtype=jnp.int32))
        return jnp.transpose(stats, (1, 0, 2)).reshape(3, groups, token_count)

    final_first = model_final(0)
    gathered_first = lax.all_gather(final_first, "exp", axis=0, tiled=True)
    final_second = model_final(1)
    gathered_second = lax.all_gather(final_second, "exp", axis=0, tiled=True)
    stats_first = model_stats(0, gathered_first)
    stats_second = model_stats(1, gathered_second)
    stacked = jnp.transpose(jnp.stack([stats_first, stats_second]), (2, 1, 0, 3))
    gathered = lax.all_to_all(stacked, "exp", 0, 0, tiled=True)
    all_max = gathered[:, 0]
    all_mass = gathered[:, 1]
    all_hit = gathered[:, 2]
    final_max = jnp.max(all_max, axis=0)
    final_mass = jnp.sum(all_mass * jnp.exp(all_max - final_max[None]), axis=0)
    final_hit = jnp.sum(all_hit, axis=0)
    token_logp = final_hit - (final_max + jnp.log(final_mass))
    difference = token_logp[0] - token_logp[1]
    seq_sums = jnp.sum(member.astype(jnp.float32) * difference[:, None], axis=0)
    devices = lax.axis_size("req") * lax.axis_size("exp")
    per_device_seqs = seq_sums.shape[0]
    everyone = devices * per_device_seqs
    dense_totals = jnp.sum(
        (owners[:, None] == jnp.arange(everyone, dtype=jnp.int32)[None, :]).astype(jnp.float32)
        * seq_sums[:, None],
        axis=0,
    )
    delivered = lax.all_to_all(
        dense_totals.reshape(devices, per_device_seqs), ("req", "exp"), 0, 0, tiled=True
    )
    seq_totals = jnp.sum(delivered, axis=0)
    return (token_logp, seq_totals)


def solution(mesh):
    in_specs = (
        P(None, ("req", "exp"), None),
        P(("req", "exp"), None),
        P("req"),
        P(None, ("req", "exp"), None),
        P(None, ("req", "exp"), None),
        P(("req", "exp")),
        P(),
        P(),
        P(),
        P(None, "exp", None, None),
        P(None, "exp", None, None),
        P(None, "exp", None),
    )
    out_specs = (P(None, ("req", "exp")), P(("req", "exp")))
    return jax.shard_map(
        per_device, mesh=mesh, in_specs=in_specs, out_specs=out_specs, check_vma=False
    )
```

```python
import jax
import jax.numpy as jnp
from jax import lax
from jax.sharding import PartitionSpec as P

HEADS = 16
KV_HEADS = 8
HEAD_DIM = 64
EXPERT_FF = 512
EXPERTS = 32
TOP = 8
CAP = 40


EPSILON = 1e-06
RESIDUAL_SCALE = 0.22
SCORE_SCALE = 0.015625
LOGIT_DIVISOR = 6.0
ROTARY_BASE = 10000.0


def combined_all(x, axis, combine):
    everything = jax.tree.map(lambda part: lax.all_gather(part, axis), x)
    initial = jax.tree.map(lambda part: part[0], everything)

    def step(k, so_far):
        return combine(so_far, jax.tree.map(lambda part: part[k], everything))

    return lax.fori_loop(1, lax.axis_size(axis), step, initial)


def root_norm(values, gain_row):
    values = values.astype(jnp.float32)
    scaled = lax.rsqrt(jnp.mean(values * values, axis=-1, keepdims=True) + EPSILON)
    return values * scaled * gain_row


def segment_table(length_row, token_count):
    seq_ends = jnp.cumsum(length_row)
    seq_starts = seq_ends - length_row
    places = jnp.arange(token_count, dtype=jnp.int32)
    segment = jnp.sum((places[:, None] >= seq_ends[None, :]).astype(jnp.int32), axis=1)
    member = segment[:, None] == jnp.arange(length_row.shape[0], dtype=jnp.int32)[None, :]
    position = places - jnp.sum(member.astype(jnp.int32) * seq_starts[None, :], axis=1)
    return (segment, member, position)


def rotary(values, position):
    half_dim = values.shape[-1] // 2
    frequency = ROTARY_BASE ** (-2.0 * jnp.arange(half_dim, dtype=jnp.float32) / values.shape[-1])
    angles = position.astype(jnp.float32)[:, None] * frequency[None, :]
    angles = jnp.concatenate([angles, angles], axis=-1)[:, None, :]
    leading = values[..., :half_dim]
    trailing = values[..., half_dim:]
    turned = jnp.concatenate([-trailing, leading], axis=-1)
    return values * jnp.cos(angles) + turned * jnp.sin(angles)


def attend(block_states, segment, position, gain_row, qkv_weight, out_weight):
    token_count = block_states.shape[0]
    group_size = HEADS // KV_HEADS
    normed = root_norm(block_states, gain_row).astype(jnp.bfloat16)
    mixed = jnp.dot(normed, qkv_weight, preferred_element_type=jnp.float32)
    queries = rotary(
        mixed[:, : HEADS * HEAD_DIM].reshape(token_count, HEADS, HEAD_DIM), position
    ).astype(jnp.bfloat16)
    keys_all = rotary(
        mixed[:, HEADS * HEAD_DIM : (HEADS + KV_HEADS) * HEAD_DIM].reshape(
            token_count, KV_HEADS, HEAD_DIM
        ),
        position,
    ).astype(jnp.bfloat16)
    values_all = (
        mixed[:, (HEADS + KV_HEADS) * HEAD_DIM :]
        .reshape(token_count, KV_HEADS, HEAD_DIM)
        .astype(jnp.bfloat16)
    )
    grouped = queries.reshape(token_count, KV_HEADS, group_size, HEAD_DIM)
    scores = (
        jnp.einsum("tgqd,sgd->gqts", grouped, keys_all, preferred_element_type=jnp.float32)
        * SCORE_SCALE
    )
    places = jnp.arange(token_count, dtype=jnp.int32)
    allowed = (segment[:, None] == segment[None, :]) & (places[None, :] <= places[:, None])
    scores = jnp.where(allowed, scores, -1e30)
    highest = jnp.max(scores, axis=-1, keepdims=True)
    weights = jnp.exp(scores - highest)
    weights = (weights / jnp.sum(weights, axis=-1, keepdims=True)).astype(jnp.bfloat16)
    attended = jnp.einsum(
        "gqts,sgd->tgqd", weights, values_all, preferred_element_type=jnp.float32
    ).astype(jnp.bfloat16)
    projected = jnp.dot(
        attended.reshape(token_count, HEADS * HEAD_DIM),
        out_weight,
        preferred_element_type=jnp.float32,
    )
    summed = block_states.astype(jnp.float32) + RESIDUAL_SCALE * projected
    return lax.reduce_precision(summed, exponent_bits=8, mantissa_bits=7).astype(jnp.bfloat16)


def join_parts(first_part, second_part):
    first_max, first_mass, first_hit = first_part
    second_max, second_mass, second_hit = second_part
    joined_max = jnp.maximum(first_max, second_max)
    joined_mass = first_mass * jnp.exp(first_max - joined_max) + second_mass * jnp.exp(
        second_max - joined_max
    )
    return (joined_max, joined_mass, first_hit + second_hit)


def per_device(
    states,
    lengths,
    targets,
    routes,
    gate_probs,
    owners,
    norm_gains,
    qkv_weight,
    out_weight,
    expert_in,
    expert_down,
    vocab_head,
):
    token_count = states.shape[1]
    width = states.shape[2]
    segment, member, position = segment_table(lengths[0], token_count)
    groups = lax.axis_size("exp")
    local_count = expert_in.shape[1]
    pairs = token_count * TOP
    slots = EXPERTS * CAP
    pair_ids = jnp.arange(pairs, dtype=jnp.int32)
    lower = (pair_ids[None, :] <= pair_ids[:, None]).astype(jnp.bfloat16)
    slot_ids = jnp.arange(slots, dtype=jnp.int32)
    shard = lax.axis_index("exp")
    vocab_rows = vocab_head.shape[1]
    lowest = shard * vocab_rows
    vocab_ids = jnp.arange(vocab_rows, dtype=jnp.int32)
    wanted_all = targets - lowest
    block_rows = 1024

    def model_final(which):
        residual = attend(
            states[which],
            segment,
            position,
            norm_gains[which, 0],
            qkv_weight[which],
            out_weight[which],
        )
        moe_in = root_norm(residual, norm_gains[which, 1]).astype(jnp.bfloat16)
        flat_routes = routes[which].reshape(pairs)
        onehot = (flat_routes[:, None] == jnp.arange(EXPERTS, dtype=jnp.int32)).astype(
            jnp.bfloat16
        )
        running = jnp.dot(lower, onehot, preferred_element_type=jnp.float32)
        rank_slot = jnp.sum((running - 1.0) * onehot.astype(jnp.float32), axis=1).astype(jnp.int32)
        local_slot = (flat_routes * CAP + rank_slot).reshape(token_count, TOP)
        chooser = jnp.sum(
            (local_slot[None, :, :] == slot_ids[:, None, None]).astype(jnp.bfloat16),
            axis=2,
            dtype=jnp.bfloat16,
        )
        outgoing = jnp.dot(chooser, moe_in, preferred_element_type=jnp.float32).astype(
            jnp.bfloat16
        )
        arrived = lax.all_to_all(
            outgoing.reshape(groups, local_count * CAP, width),
            "exp",
            split_axis=0,
            concat_axis=0,
            tiled=True,
        )
        inputs = arrived.reshape(groups, local_count, CAP, width)
        gate_up = jnp.einsum(
            "slcd,ldf->slcf", inputs, expert_in[which], preferred_element_type=jnp.float32
        )
        hidden = (jax.nn.silu(gate_up[..., :EXPERT_FF]) * gate_up[..., EXPERT_FF:]).astype(
            jnp.bfloat16
        )
        produced = jnp.einsum(
            "slcf,lfd->slcd", hidden, expert_down[which], preferred_element_type=jnp.float32
        ).astype(jnp.bfloat16)
        returned = lax.all_to_all(
            produced.reshape(groups, local_count * CAP, width),
            "exp",
            split_axis=0,
            concat_axis=0,
            tiled=True,
        ).reshape(slots, width)
        picker = (local_slot[..., None] == slot_ids[None, None, :]).astype(jnp.bfloat16)
        picked = jnp.einsum("tks,sd->tkd", picker, returned, preferred_element_type=jnp.float32)
        mixture = jnp.sum(gate_probs[which][..., None] * picked, axis=1)
        final = root_norm(
            residual.astype(jnp.float32) + RESIDUAL_SCALE * mixture, norm_gains[which, 2]
        ).astype(jnp.bfloat16)
        return final

    def model_stats(which, chunk):
        chunk_rows = chunk.shape[0]
        block_count = chunk_rows // block_rows
        head = vocab_head[which]

        def one_block(block_number):
            row_block = lax.dynamic_slice_in_dim(chunk, block_number * block_rows, block_rows, 0)
            wanted = lax.dynamic_slice_in_dim(wanted_all, block_number * block_rows, block_rows, 0)
            logits = (
                jnp.einsum("td,vd->tv", row_block, head, preferred_element_type=jnp.float32)
                / LOGIT_DIVISOR
            )
            highest = jnp.max(logits, axis=1)
            masses = jnp.sum(jnp.exp(logits - highest[:, None]), axis=1)
            chosen = jnp.sum(jnp.where(wanted[:, None] == vocab_ids[None, :], logits, 0.0), axis=1)
            return jnp.stack([highest, masses, chosen])

        stats = lax.map(one_block, jnp.arange(block_count, dtype=jnp.int32))
        return jnp.transpose(stats, (1, 0, 2)).reshape(3, groups, token_count)

    final_first = model_final(0)
    gathered_first = lax.all_gather(final_first, "exp", axis=0, tiled=True)
    final_second = model_final(1)
    gathered_second = lax.all_gather(final_second, "exp", axis=0, tiled=True)
    stats_first = model_stats(0, gathered_first)
    stats_second = model_stats(1, gathered_second)
    stacked = jnp.transpose(jnp.stack([stats_first, stats_second]), (2, 1, 0, 3))
    gathered = lax.all_to_all(stacked, "exp", 0, 0, tiled=True)
    all_max = gathered[:, 0]
    all_mass = gathered[:, 1]
    all_hit = gathered[:, 2]
    final_max = jnp.max(all_max, axis=0)
    final_mass = jnp.sum(all_mass * jnp.exp(all_max - final_max[None]), axis=0)
    final_hit = jnp.sum(all_hit, axis=0)
    token_logp = final_hit - (final_max + jnp.log(final_mass))
    difference = token_logp[0] - token_logp[1]
    seq_sums = jnp.sum(member.astype(jnp.float32) * difference[:, None], axis=0)
    devices = lax.axis_size("req") * lax.axis_size("exp")
    per_device_seqs = seq_sums.shape[0]
    everyone = devices * per_device_seqs
    dense_totals = jnp.sum(
        (owners[:, None] == jnp.arange(everyone, dtype=jnp.int32)[None, :]).astype(jnp.float32)
        * seq_sums[:, None],
        axis=0,
    )
    delivered = lax.all_to_all(
        dense_totals.reshape(devices, per_device_seqs), ("req", "exp"), 0, 0, tiled=True
    )
    seq_totals = jnp.sum(delivered, axis=0)
    return (token_logp, seq_totals)


def solution(mesh):
    in_specs = (
        P(None, ("req", "exp"), None),
        P(("req", "exp"), None),
        P("req"),
        P(None, ("req", "exp"), None),
        P(None, ("req", "exp"), None),
        P(("req", "exp")),
        P(),
        P(),
        P(),
        P(None, "exp", None, None),
        P(None, "exp", None, None),
        P(None, "exp", None),
    )
    out_specs = (P(None, ("req", "exp")), P(("req", "exp")))
    return jax.shard_map(
        per_device, mesh=mesh, in_specs=in_specs, out_specs=out_specs, check_vma=False
    )
```

```python
import jax
import jax.numpy as jnp
from jax import lax
from jax.sharding import PartitionSpec as P

HEADS = 16
KV_HEADS = 8
HEAD_DIM = 64
EXPERT_FF = 512
EXPERTS = 32
TOP = 8
CAP = 40


EPSILON = 1e-06
RESIDUAL_SCALE = 0.22
SCORE_SCALE = 0.015625
LOGIT_DIVISOR = 6.0
ROTARY_BASE = 10000.0


def combined_all(x, axis, combine):
    everything = jax.tree.map(lambda part: lax.all_gather(part, axis), x)
    initial = jax.tree.map(lambda part: part[0], everything)

    def step(k, so_far):
        return combine(so_far, jax.tree.map(lambda part: part[k], everything))

    return lax.fori_loop(1, lax.axis_size(axis), step, initial)


def root_norm(values, gain_row):
    values = values.astype(jnp.float32)
    scaled = lax.rsqrt(jnp.mean(values * values, axis=-1, keepdims=True) + EPSILON)
    return values * scaled * gain_row


def segment_table(length_row, token_count):
    seq_ends = jnp.cumsum(length_row)
    seq_starts = seq_ends - length_row
    places = jnp.arange(token_count, dtype=jnp.int32)
    segment = jnp.sum((places[:, None] >= seq_ends[None, :]).astype(jnp.int32), axis=1)
    member = segment[:, None] == jnp.arange(length_row.shape[0], dtype=jnp.int32)[None, :]
    position = places - jnp.sum(member.astype(jnp.int32) * seq_starts[None, :], axis=1)
    return (segment, member, position)


def rotary(values, position):
    half_dim = values.shape[-1] // 2
    frequency = ROTARY_BASE ** (-2.0 * jnp.arange(half_dim, dtype=jnp.float32) / values.shape[-1])
    angles = position.astype(jnp.float32)[:, None] * frequency[None, :]
    angles = jnp.concatenate([angles, angles], axis=-1)[:, None, :]
    leading = values[..., :half_dim]
    trailing = values[..., half_dim:]
    turned = jnp.concatenate([-trailing, leading], axis=-1)
    return values * jnp.cos(angles) + turned * jnp.sin(angles)


def attend(block_states, segment, position, gain_row, qkv_weight, out_weight):
    token_count = block_states.shape[0]
    group_size = HEADS // KV_HEADS
    normed = root_norm(block_states, gain_row).astype(jnp.bfloat16)
    mixed = jnp.dot(normed, qkv_weight, preferred_element_type=jnp.float32)
    queries = rotary(
        mixed[:, : HEADS * HEAD_DIM].reshape(token_count, HEADS, HEAD_DIM), position
    ).astype(jnp.bfloat16)
    keys_all = rotary(
        mixed[:, HEADS * HEAD_DIM : (HEADS + KV_HEADS) * HEAD_DIM].reshape(
            token_count, KV_HEADS, HEAD_DIM
        ),
        position,
    ).astype(jnp.bfloat16)
    values_all = (
        mixed[:, (HEADS + KV_HEADS) * HEAD_DIM :]
        .reshape(token_count, KV_HEADS, HEAD_DIM)
        .astype(jnp.bfloat16)
    )
    grouped = queries.reshape(token_count, KV_HEADS, group_size, HEAD_DIM)
    scores = (
        jnp.einsum("tgqd,sgd->gqts", grouped, keys_all, preferred_element_type=jnp.float32)
        * SCORE_SCALE
    )
    places = jnp.arange(token_count, dtype=jnp.int32)
    allowed = (segment[:, None] == segment[None, :]) & (places[None, :] <= places[:, None])
    scores = jnp.where(allowed, scores, -1e30)
    highest = jnp.max(scores, axis=-1, keepdims=True)
    weights = jnp.exp(scores - highest)
    weights = (weights / jnp.sum(weights, axis=-1, keepdims=True)).astype(jnp.bfloat16)
    attended = jnp.einsum(
        "gqts,sgd->tgqd", weights, values_all, preferred_element_type=jnp.float32
    ).astype(jnp.bfloat16)
    projected = jnp.dot(
        attended.reshape(token_count, HEADS * HEAD_DIM),
        out_weight,
        preferred_element_type=jnp.float32,
    )
    summed = block_states.astype(jnp.float32) + RESIDUAL_SCALE * projected
    return lax.reduce_precision(summed, exponent_bits=8, mantissa_bits=7).astype(jnp.bfloat16)


def join_parts(first_part, second_part):
    first_max, first_mass, first_hit = first_part
    second_max, second_mass, second_hit = second_part
    joined_max = jnp.maximum(first_max, second_max)
    joined_mass = first_mass * jnp.exp(first_max - joined_max) + second_mass * jnp.exp(
        second_max - joined_max
    )
    return (joined_max, joined_mass, first_hit + second_hit)


def per_device(
    states,
    lengths,
    targets,
    routes,
    gate_probs,
    owners,
    norm_gains,
    qkv_weight,
    out_weight,
    expert_in,
    expert_down,
    vocab_head,
):
    token_count = states.shape[1]
    width = states.shape[2]
    segment, member, position = segment_table(lengths[0], token_count)
    groups = lax.axis_size("exp")
    local_count = expert_in.shape[1]
    pairs = token_count * TOP
    slots = EXPERTS * CAP
    pair_ids = jnp.arange(pairs, dtype=jnp.int32)
    lower = (pair_ids[None, :] <= pair_ids[:, None]).astype(jnp.bfloat16)
    slot_ids = jnp.arange(slots, dtype=jnp.int32)
    shard = lax.axis_index("exp")
    vocab_rows = vocab_head.shape[1]
    lowest = shard * vocab_rows
    vocab_ids = jnp.arange(vocab_rows, dtype=jnp.int32)
    wanted_all = targets - lowest
    block_rows = 1024

    def model_entry(which):
        residual = attend(
            states[which],
            segment,
            position,
            norm_gains[which, 0],
            qkv_weight[which],
            out_weight[which],
        )
        moe_in = root_norm(residual, norm_gains[which, 1]).astype(jnp.bfloat16)
        flat_routes = routes[which].reshape(pairs)
        onehot = (flat_routes[:, None] == jnp.arange(EXPERTS, dtype=jnp.int32)).astype(
            jnp.bfloat16
        )
        running = jnp.dot(lower, onehot, preferred_element_type=jnp.float32)
        rank_slot = jnp.sum((running - 1.0) * onehot.astype(jnp.float32), axis=1).astype(jnp.int32)
        local_slot = (flat_routes * CAP + rank_slot).reshape(token_count, TOP)
        chooser = jnp.sum(
            (local_slot[None, :, :] == slot_ids[:, None, None]).astype(jnp.bfloat16),
            axis=2,
            dtype=jnp.bfloat16,
        )
        outgoing = jnp.dot(chooser, moe_in, preferred_element_type=jnp.float32).astype(
            jnp.bfloat16
        )
        return residual, local_slot, outgoing.reshape(groups, local_count * CAP, width)

    def model_experts(which, arrived):
        inputs = arrived.reshape(groups, local_count, CAP, width)
        gate_up = jnp.einsum(
            "slcd,ldf->slcf", inputs, expert_in[which], preferred_element_type=jnp.float32
        )
        hidden = (jax.nn.silu(gate_up[..., :EXPERT_FF]) * gate_up[..., EXPERT_FF:]).astype(
            jnp.bfloat16
        )
        produced = jnp.einsum(
            "slcf,lfd->slcd", hidden, expert_down[which], preferred_element_type=jnp.float32
        ).astype(jnp.bfloat16)
        return produced.reshape(groups, local_count * CAP, width)

    def model_exit(which, residual, local_slot, returned):
        returned = returned.reshape(slots, width)
        picker = (local_slot[..., None] == slot_ids[None, None, :]).astype(jnp.bfloat16)
        picked = jnp.einsum("tks,sd->tkd", picker, returned, preferred_element_type=jnp.float32)
        mixture = jnp.sum(gate_probs[which][..., None] * picked, axis=1)
        final = root_norm(
            residual.astype(jnp.float32) + RESIDUAL_SCALE * mixture, norm_gains[which, 2]
        ).astype(jnp.bfloat16)
        return final

    def exchange(blocks):
        return lax.all_to_all(blocks, "exp", split_axis=0, concat_axis=0, tiled=True)

    def model_stats(which, chunk):
        chunk_rows = chunk.shape[0]
        block_count = chunk_rows // block_rows
        head = vocab_head[which]

        def one_block(block_number):
            row_block = lax.dynamic_slice_in_dim(chunk, block_number * block_rows, block_rows, 0)
            wanted = lax.dynamic_slice_in_dim(wanted_all, block_number * block_rows, block_rows, 0)
            logits = (
                jnp.einsum("td,vd->tv", row_block, head, preferred_element_type=jnp.float32)
                / LOGIT_DIVISOR
            )
            highest = jnp.max(logits, axis=1)
            masses = jnp.sum(jnp.exp(logits - highest[:, None]), axis=1)
            chosen = jnp.sum(jnp.where(wanted[:, None] == vocab_ids[None, :], logits, 0.0), axis=1)
            return jnp.stack([highest, masses, chosen])

        stats = lax.map(one_block, jnp.arange(block_count, dtype=jnp.int32))
        return jnp.transpose(stats, (1, 0, 2)).reshape(3, groups, token_count)

    row_span = local_count * CAP
    residual_first, slot_first, outgoing_first = model_entry(0)
    produced_first = model_experts(0, exchange(outgoing_first))
    residual_second, slot_second, outgoing_second = model_entry(1)
    crossed = exchange(jnp.concatenate([produced_first, outgoing_second], axis=1))
    final_first = model_exit(0, residual_first, slot_first, crossed[:, :row_span])
    gathered_first = lax.all_gather(final_first, "exp", axis=0, tiled=True)
    produced_second = model_experts(1, crossed[:, row_span:])
    final_second = model_exit(1, residual_second, slot_second, exchange(produced_second))
    gathered_second = lax.all_gather(final_second, "exp", axis=0, tiled=True)
    stats_first = model_stats(0, gathered_first)
    stats_second = model_stats(1, gathered_second)
    stacked = jnp.transpose(jnp.stack([stats_first, stats_second]), (2, 1, 0, 3))
    gathered = lax.all_to_all(stacked, "exp", 0, 0, tiled=True)
    all_max = gathered[:, 0]
    all_mass = gathered[:, 1]
    all_hit = gathered[:, 2]
    final_max = jnp.max(all_max, axis=0)
    final_mass = jnp.sum(all_mass * jnp.exp(all_max - final_max[None]), axis=0)
    final_hit = jnp.sum(all_hit, axis=0)
    token_logp = final_hit - (final_max + jnp.log(final_mass))
    difference = token_logp[0] - token_logp[1]
    seq_sums = jnp.sum(member.astype(jnp.float32) * difference[:, None], axis=0)
    devices = lax.axis_size("req") * lax.axis_size("exp")
    per_device_seqs = seq_sums.shape[0]
    everyone = devices * per_device_seqs
    dense_totals = jnp.sum(
        (owners[:, None] == jnp.arange(everyone, dtype=jnp.int32)[None, :]).astype(jnp.float32)
        * seq_sums[:, None],
        axis=0,
    )
    delivered = lax.all_to_all(
        dense_totals.reshape(devices, per_device_seqs), ("req", "exp"), 0, 0, tiled=True
    )
    seq_totals = jnp.sum(delivered, axis=0)
    return (token_logp, seq_totals)


def solution(mesh):
    in_specs = (
        P(None, ("req", "exp"), None),
        P(("req", "exp"), None),
        P("req"),
        P(None, ("req", "exp"), None),
        P(None, ("req", "exp"), None),
        P(("req", "exp")),
        P(),
        P(),
        P(),
        P(None, "exp", None, None),
        P(None, "exp", None, None),
        P(None, "exp", None),
    )
    out_specs = (P(None, ("req", "exp")), P(("req", "exp")))
    return jax.shard_map(
        per_device, mesh=mesh, in_specs=in_specs, out_specs=out_specs, check_vma=False
    )
```

```python
import jax
import jax.numpy as jnp
from jax import lax
from jax.sharding import PartitionSpec as P

HEADS = 16
KV_HEADS = 8
HEAD_DIM = 64
EXPERT_FF = 512
EXPERTS = 32
TOP = 8
CAP = 40


EPSILON = 1e-06
RESIDUAL_SCALE = 0.22
SCORE_SCALE = 0.015625
LOGIT_DIVISOR = 6.0
ROTARY_BASE = 10000.0


def combined_all(x, axis, combine):
    everything = jax.tree.map(lambda part: lax.all_gather(part, axis), x)
    initial = jax.tree.map(lambda part: part[0], everything)

    def step(k, so_far):
        return combine(so_far, jax.tree.map(lambda part: part[k], everything))

    return lax.fori_loop(1, lax.axis_size(axis), step, initial)


def root_norm(values, gain_row):
    values = values.astype(jnp.float32)
    scaled = lax.rsqrt(jnp.mean(values * values, axis=-1, keepdims=True) + EPSILON)
    return values * scaled * gain_row


def segment_table(length_row, token_count):
    seq_ends = jnp.cumsum(length_row)
    seq_starts = seq_ends - length_row
    places = jnp.arange(token_count, dtype=jnp.int32)
    segment = jnp.sum((places[:, None] >= seq_ends[None, :]).astype(jnp.int32), axis=1)
    member = segment[:, None] == jnp.arange(length_row.shape[0], dtype=jnp.int32)[None, :]
    position = places - jnp.sum(member.astype(jnp.int32) * seq_starts[None, :], axis=1)
    return (segment, member, position)


def rotary(values, position):
    half_dim = values.shape[-1] // 2
    frequency = ROTARY_BASE ** (-2.0 * jnp.arange(half_dim, dtype=jnp.float32) / values.shape[-1])
    angles = position.astype(jnp.float32)[:, None] * frequency[None, :]
    angles = jnp.concatenate([angles, angles], axis=-1)[:, None, :]
    leading = values[..., :half_dim]
    trailing = values[..., half_dim:]
    turned = jnp.concatenate([-trailing, leading], axis=-1)
    return values * jnp.cos(angles) + turned * jnp.sin(angles)


def attend(block_states, segment, position, gain_row, qkv_weight, out_weight):
    token_count = block_states.shape[0]
    group_size = HEADS // KV_HEADS
    normed = root_norm(block_states, gain_row).astype(jnp.bfloat16)
    mixed = jnp.dot(normed, qkv_weight, preferred_element_type=jnp.float32)
    queries = rotary(
        mixed[:, : HEADS * HEAD_DIM].reshape(token_count, HEADS, HEAD_DIM), position
    ).astype(jnp.bfloat16)
    keys_all = rotary(
        mixed[:, HEADS * HEAD_DIM : (HEADS + KV_HEADS) * HEAD_DIM].reshape(
            token_count, KV_HEADS, HEAD_DIM
        ),
        position,
    ).astype(jnp.bfloat16)
    values_all = (
        mixed[:, (HEADS + KV_HEADS) * HEAD_DIM :]
        .reshape(token_count, KV_HEADS, HEAD_DIM)
        .astype(jnp.bfloat16)
    )
    grouped = queries.reshape(token_count, KV_HEADS, group_size, HEAD_DIM)
    scores = (
        jnp.einsum("tgqd,sgd->gqts", grouped, keys_all, preferred_element_type=jnp.float32)
        * SCORE_SCALE
    )
    places = jnp.arange(token_count, dtype=jnp.int32)
    allowed = (segment[:, None] == segment[None, :]) & (places[None, :] <= places[:, None])
    scores = jnp.where(allowed, scores, -1e30)
    highest = jnp.max(scores, axis=-1, keepdims=True)
    weights = jnp.exp(scores - highest)
    weights = (weights / jnp.sum(weights, axis=-1, keepdims=True)).astype(jnp.bfloat16)
    attended = jnp.einsum(
        "gqts,sgd->tgqd", weights, values_all, preferred_element_type=jnp.float32
    ).astype(jnp.bfloat16)
    projected = jnp.dot(
        attended.reshape(token_count, HEADS * HEAD_DIM),
        out_weight,
        preferred_element_type=jnp.float32,
    )
    summed = block_states.astype(jnp.float32) + RESIDUAL_SCALE * projected
    return lax.reduce_precision(summed, exponent_bits=8, mantissa_bits=7).astype(jnp.bfloat16)


def join_parts(first_part, second_part):
    first_max, first_mass, first_hit = first_part
    second_max, second_mass, second_hit = second_part
    joined_max = jnp.maximum(first_max, second_max)
    joined_mass = first_mass * jnp.exp(first_max - joined_max) + second_mass * jnp.exp(
        second_max - joined_max
    )
    return (joined_max, joined_mass, first_hit + second_hit)


def per_device(
    states,
    lengths,
    targets,
    routes,
    gate_probs,
    owners,
    norm_gains,
    qkv_weight,
    out_weight,
    expert_in,
    expert_down,
    vocab_head,
):
    token_count = states.shape[1]
    width = states.shape[2]
    segment, member, position = segment_table(lengths[0], token_count)
    groups = lax.axis_size("exp")
    local_count = expert_in.shape[1]
    pairs = token_count * TOP
    slots = EXPERTS * CAP
    pair_ids = jnp.arange(pairs, dtype=jnp.int32)
    lower = (pair_ids[None, :] <= pair_ids[:, None]).astype(jnp.bfloat16)
    slot_ids = jnp.arange(slots, dtype=jnp.int32)
    shard = lax.axis_index("exp")
    vocab_rows = vocab_head.shape[1]
    lowest = shard * vocab_rows
    vocab_ids = jnp.arange(vocab_rows, dtype=jnp.int32)
    wanted_all = targets - lowest
    block_rows = 1024

    def model_entry(which):
        residual = attend(
            states[which],
            segment,
            position,
            norm_gains[which, 0],
            qkv_weight[which],
            out_weight[which],
        )
        moe_in = root_norm(residual, norm_gains[which, 1]).astype(jnp.bfloat16)
        flat_routes = routes[which].reshape(pairs)
        onehot = (flat_routes[:, None] == jnp.arange(EXPERTS, dtype=jnp.int32)).astype(
            jnp.bfloat16
        )
        running = jnp.dot(lower, onehot, preferred_element_type=jnp.float32)
        rank_slot = jnp.sum((running - 1.0) * onehot.astype(jnp.float32), axis=1).astype(jnp.int32)
        local_slot = (flat_routes * CAP + rank_slot).reshape(token_count, TOP)
        chooser = (local_slot.reshape(pairs)[:, None] == slot_ids[None, :]).astype(jnp.bfloat16)
        repeated = jnp.repeat(moe_in, TOP, axis=0)
        outgoing = jnp.einsum(
            "ps,pd->sd", chooser, repeated, preferred_element_type=jnp.float32
        ).astype(jnp.bfloat16)
        return residual, local_slot, outgoing.reshape(groups, local_count * CAP, width)

    def model_experts(which, arrived):
        inputs = arrived.reshape(groups, local_count, CAP, width)
        gate_up = jnp.einsum(
            "slcd,ldf->slcf", inputs, expert_in[which], preferred_element_type=jnp.float32
        )
        hidden = (jax.nn.silu(gate_up[..., :EXPERT_FF]) * gate_up[..., EXPERT_FF:]).astype(
            jnp.bfloat16
        )
        produced = jnp.einsum(
            "slcf,lfd->slcd", hidden, expert_down[which], preferred_element_type=jnp.float32
        ).astype(jnp.bfloat16)
        return produced.reshape(groups, local_count * CAP, width)

    def model_exit(which, residual, local_slot, returned):
        returned = returned.reshape(slots, width)
        picker = (local_slot[..., None] == slot_ids[None, None, :]).astype(jnp.bfloat16)
        picked = jnp.einsum("tks,sd->tkd", picker, returned, preferred_element_type=jnp.float32)
        mixture = jnp.sum(gate_probs[which][..., None] * picked, axis=1)
        final = root_norm(
            residual.astype(jnp.float32) + RESIDUAL_SCALE * mixture, norm_gains[which, 2]
        ).astype(jnp.bfloat16)
        return final

    def exchange(blocks):
        return lax.all_to_all(blocks, "exp", split_axis=0, concat_axis=0, tiled=True)

    def model_stats(which, chunk):
        chunk_rows = chunk.shape[0]
        block_count = chunk_rows // block_rows
        def one_block(block_number):
            head = vocab_head[which]
            row_block = lax.dynamic_slice_in_dim(chunk, block_number * block_rows, block_rows, 0)
            wanted = lax.dynamic_slice_in_dim(wanted_all, block_number * block_rows, block_rows, 0)
            logits = (
                jnp.einsum("td,vd->tv", row_block, head, preferred_element_type=jnp.float32)
                / LOGIT_DIVISOR
            )
            highest = jnp.max(logits, axis=1)
            masses = jnp.sum(jnp.exp(logits - highest[:, None]), axis=1)
            chosen = jnp.sum(jnp.where(wanted[:, None] == vocab_ids[None, :], logits, 0.0), axis=1)
            return jnp.stack([highest, masses, chosen])

        stats = lax.map(one_block, jnp.arange(block_count, dtype=jnp.int32))
        return jnp.transpose(stats, (1, 0, 2)).reshape(3, groups, token_count)

    row_span = local_count * CAP
    residual_first, slot_first, outgoing_first = model_entry(0)
    produced_first = model_experts(0, exchange(outgoing_first))
    residual_second, slot_second, outgoing_second = model_entry(1)
    crossed = exchange(jnp.concatenate([produced_first, outgoing_second], axis=1))
    final_first = model_exit(0, residual_first, slot_first, crossed[:, :row_span])
    gathered_first = lax.all_gather(final_first, "exp", axis=0, tiled=True)
    produced_second = model_experts(1, crossed[:, row_span:])
    final_second = model_exit(1, residual_second, slot_second, exchange(produced_second))
    gathered_second = lax.all_gather(final_second, "exp", axis=0, tiled=True)
    stats_first = model_stats(0, gathered_first)
    stats_second = model_stats(1, gathered_second)
    stacked = jnp.transpose(jnp.stack([stats_first, stats_second]), (2, 1, 0, 3))
    gathered = lax.all_to_all(stacked, "exp", 0, 0, tiled=True)
    all_max = gathered[:, 0]
    all_mass = gathered[:, 1]
    all_hit = gathered[:, 2]
    final_max = jnp.max(all_max, axis=0)
    final_mass = jnp.sum(all_mass * jnp.exp(all_max - final_max[None]), axis=0)
    final_hit = jnp.sum(all_hit, axis=0)
    token_logp = final_hit - (final_max + jnp.log(final_mass))
    difference = token_logp[0] - token_logp[1]
    seq_sums = jnp.sum(member.astype(jnp.float32) * difference[:, None], axis=0)
    devices = lax.axis_size("req") * lax.axis_size("exp")
    per_device_seqs = seq_sums.shape[0]
    everyone = devices * per_device_seqs
    dense_totals = jnp.sum(
        (owners[:, None] == jnp.arange(everyone, dtype=jnp.int32)[None, :]).astype(jnp.float32)
        * seq_sums[:, None],
        axis=0,
    )
    delivered = lax.all_to_all(
        dense_totals.reshape(devices, per_device_seqs), ("req", "exp"), 0, 0, tiled=True
    )
    seq_totals = jnp.sum(delivered, axis=0)
    return (token_logp, seq_totals)


def solution(mesh):
    in_specs = (
        P(None, ("req", "exp"), None),
        P(("req", "exp"), None),
        P("req"),
        P(None, ("req", "exp"), None),
        P(None, ("req", "exp"), None),
        P(("req", "exp")),
        P(),
        P(),
        P(),
        P(None, "exp", None, None),
        P(None, "exp", None, None),
        P(None, "exp", None),
    )
    out_specs = (P(None, ("req", "exp")), P(("req", "exp")))
    return jax.shard_map(
        per_device, mesh=mesh, in_specs=in_specs, out_specs=out_specs, check_vma=False
    )
```

```python
import jax
import jax.numpy as jnp
from jax import lax
from jax.sharding import PartitionSpec as P

HEADS = 16
KV_HEADS = 8
HEAD_DIM = 64
EXPERT_FF = 512
EXPERTS = 32
TOP = 8
CAP = 40


EPSILON = 1e-06
RESIDUAL_SCALE = 0.22
SCORE_SCALE = 0.015625
LOGIT_DIVISOR = 6.0
ROTARY_BASE = 10000.0


def combined_all(x, axis, combine):
    everything = jax.tree.map(lambda part: lax.all_gather(part, axis), x)
    initial = jax.tree.map(lambda part: part[0], everything)

    def step(k, so_far):
        return combine(so_far, jax.tree.map(lambda part: part[k], everything))

    return lax.fori_loop(1, lax.axis_size(axis), step, initial)


def root_norm(values, gain_row):
    values = values.astype(jnp.float32)
    scaled = lax.rsqrt(jnp.mean(values * values, axis=-1, keepdims=True) + EPSILON)
    return values * scaled * gain_row


def segment_table(length_row, token_count):
    seq_ends = jnp.cumsum(length_row)
    seq_starts = seq_ends - length_row
    places = jnp.arange(token_count, dtype=jnp.int32)
    segment = jnp.sum((places[:, None] >= seq_ends[None, :]).astype(jnp.int32), axis=1)
    member = segment[:, None] == jnp.arange(length_row.shape[0], dtype=jnp.int32)[None, :]
    position = places - jnp.sum(member.astype(jnp.int32) * seq_starts[None, :], axis=1)
    return (segment, member, position)


def rotary(values, position):
    half_dim = values.shape[-1] // 2
    frequency = ROTARY_BASE ** (-2.0 * jnp.arange(half_dim, dtype=jnp.float32) / values.shape[-1])
    angles = position.astype(jnp.float32)[:, None] * frequency[None, :]
    angles = jnp.concatenate([angles, angles], axis=-1)[:, None, :]
    leading = values[..., :half_dim]
    trailing = values[..., half_dim:]
    turned = jnp.concatenate([-trailing, leading], axis=-1)
    return values * jnp.cos(angles) + turned * jnp.sin(angles)


def attend(block_states, segment, position, gain_row, qkv_weight, out_weight):
    token_count = block_states.shape[0]
    group_size = HEADS // KV_HEADS
    normed = root_norm(block_states, gain_row).astype(jnp.bfloat16)
    mixed = jnp.dot(normed, qkv_weight, preferred_element_type=jnp.float32)
    queries = rotary(
        mixed[:, : HEADS * HEAD_DIM].reshape(token_count, HEADS, HEAD_DIM), position
    ).astype(jnp.bfloat16)
    keys_all = rotary(
        mixed[:, HEADS * HEAD_DIM : (HEADS + KV_HEADS) * HEAD_DIM].reshape(
            token_count, KV_HEADS, HEAD_DIM
        ),
        position,
    ).astype(jnp.bfloat16)
    values_all = (
        mixed[:, (HEADS + KV_HEADS) * HEAD_DIM :]
        .reshape(token_count, KV_HEADS, HEAD_DIM)
        .astype(jnp.bfloat16)
    )
    grouped = queries.reshape(token_count, KV_HEADS, group_size, HEAD_DIM)
    scores = (
        jnp.einsum("tgqd,sgd->gqts", grouped, keys_all, preferred_element_type=jnp.float32)
        * SCORE_SCALE
    )
    places = jnp.arange(token_count, dtype=jnp.int32)
    allowed = (segment[:, None] == segment[None, :]) & (places[None, :] <= places[:, None])
    scores = jnp.where(allowed, scores, -1e30)
    highest = jnp.max(scores, axis=-1, keepdims=True)
    weights = jnp.exp(scores - highest)
    weights = (weights / jnp.sum(weights, axis=-1, keepdims=True)).astype(jnp.bfloat16)
    attended = jnp.einsum(
        "gqts,sgd->tgqd", weights, values_all, preferred_element_type=jnp.float32
    ).astype(jnp.bfloat16)
    projected = jnp.dot(
        attended.reshape(token_count, HEADS * HEAD_DIM),
        out_weight,
        preferred_element_type=jnp.float32,
    )
    summed = block_states.astype(jnp.float32) + RESIDUAL_SCALE * projected
    return lax.reduce_precision(summed, exponent_bits=8, mantissa_bits=7).astype(jnp.bfloat16)


def join_parts(first_part, second_part):
    first_max, first_mass, first_hit = first_part
    second_max, second_mass, second_hit = second_part
    joined_max = jnp.maximum(first_max, second_max)
    joined_mass = first_mass * jnp.exp(first_max - joined_max) + second_mass * jnp.exp(
        second_max - joined_max
    )
    return (joined_max, joined_mass, first_hit + second_hit)


def per_device(
    states,
    lengths,
    targets,
    routes,
    gate_probs,
    owners,
    norm_gains,
    qkv_weight,
    out_weight,
    expert_in,
    expert_down,
    vocab_head,
):
    token_count = states.shape[1]
    width = states.shape[2]
    segment, member, position = segment_table(lengths[0], token_count)
    groups = lax.axis_size("exp")
    local_count = expert_in.shape[1]
    pairs = token_count * TOP
    slots = EXPERTS * CAP
    pair_ids = jnp.arange(pairs, dtype=jnp.int32)
    lower = (pair_ids[None, :] <= pair_ids[:, None]).astype(jnp.bfloat16)
    slot_ids = jnp.arange(slots, dtype=jnp.int32)
    shard = lax.axis_index("exp")
    vocab_rows = vocab_head.shape[1]
    lowest = shard * vocab_rows
    vocab_ids = jnp.arange(vocab_rows, dtype=jnp.int32)
    wanted_all = targets - lowest
    block_rows = 2048

    def model_entry(which):
        residual = attend(
            states[which],
            segment,
            position,
            norm_gains[which, 0],
            qkv_weight[which],
            out_weight[which],
        )
        moe_in = root_norm(residual, norm_gains[which, 1]).astype(jnp.bfloat16)
        flat_routes = routes[which].reshape(pairs)
        onehot = (flat_routes[:, None] == jnp.arange(EXPERTS, dtype=jnp.int32)).astype(
            jnp.bfloat16
        )
        running = jnp.dot(lower, onehot, preferred_element_type=jnp.float32)
        rank_slot = jnp.sum((running - 1.0) * onehot.astype(jnp.float32), axis=1).astype(jnp.int32)
        local_slot = (flat_routes * CAP + rank_slot).reshape(token_count, TOP)
        chooser = (local_slot.reshape(pairs)[:, None] == slot_ids[None, :]).astype(jnp.bfloat16)
        repeated = jnp.repeat(moe_in, TOP, axis=0)
        outgoing = jnp.einsum(
            "ps,pd->sd", chooser, repeated, preferred_element_type=jnp.float32
        ).astype(jnp.bfloat16)
        return residual, local_slot, outgoing.reshape(groups, local_count * CAP, width)

    def model_experts(which, arrived):
        inputs = arrived.reshape(groups, local_count, CAP, width)
        gate_up = jnp.einsum(
            "slcd,ldf->slcf", inputs, expert_in[which], preferred_element_type=jnp.float32
        )
        hidden = (jax.nn.silu(gate_up[..., :EXPERT_FF]) * gate_up[..., EXPERT_FF:]).astype(
            jnp.bfloat16
        )
        produced = jnp.einsum(
            "slcf,lfd->slcd", hidden, expert_down[which], preferred_element_type=jnp.float32
        ).astype(jnp.bfloat16)
        return produced.reshape(groups, local_count * CAP, width)

    def model_exit(which, residual, local_slot, returned):
        returned = returned.reshape(slots, width)
        picker = (local_slot[..., None] == slot_ids[None, None, :]).astype(jnp.bfloat16)
        picked = jnp.einsum("tks,sd->tkd", picker, returned, preferred_element_type=jnp.float32)
        mixture = jnp.sum(gate_probs[which][..., None] * picked, axis=1)
        final = root_norm(
            residual.astype(jnp.float32) + RESIDUAL_SCALE * mixture, norm_gains[which, 2]
        ).astype(jnp.bfloat16)
        return final

    def exchange(blocks):
        return lax.all_to_all(blocks, "exp", split_axis=0, concat_axis=0, tiled=True)

    def model_stats(which, chunk):
        chunk_rows = chunk.shape[0]
        block_count = chunk_rows // block_rows
        def one_block(block_number):
            head = vocab_head[which]
            row_block = lax.dynamic_slice_in_dim(chunk, block_number * block_rows, block_rows, 0)
            wanted = lax.dynamic_slice_in_dim(wanted_all, block_number * block_rows, block_rows, 0)
            logits = (
                jnp.einsum("td,vd->tv", row_block, head, preferred_element_type=jnp.float32)
                / LOGIT_DIVISOR
            )
            highest = jnp.max(logits, axis=1)
            masses = jnp.sum(jnp.exp(logits - highest[:, None]), axis=1)
            chosen = jnp.sum(jnp.where(wanted[:, None] == vocab_ids[None, :], logits, 0.0), axis=1)
            return jnp.stack([highest, masses, chosen])

        stats = lax.map(one_block, jnp.arange(block_count, dtype=jnp.int32))
        return jnp.transpose(stats, (1, 0, 2)).reshape(3, groups, token_count)

    row_span = local_count * CAP
    residual_first, slot_first, outgoing_first = model_entry(0)
    produced_first = model_experts(0, exchange(outgoing_first))
    residual_second, slot_second, outgoing_second = model_entry(1)
    crossed = exchange(jnp.concatenate([produced_first, outgoing_second], axis=1))
    final_first = model_exit(0, residual_first, slot_first, crossed[:, :row_span])
    gathered_first = lax.all_gather(final_first, "exp", axis=0, tiled=True)
    produced_second = model_experts(1, crossed[:, row_span:])
    final_second = model_exit(1, residual_second, slot_second, exchange(produced_second))
    gathered_second = lax.all_gather(final_second, "exp", axis=0, tiled=True)
    stats_first = model_stats(0, gathered_first)
    stats_second = model_stats(1, gathered_second)
    stacked = jnp.transpose(jnp.stack([stats_first, stats_second]), (2, 1, 0, 3))
    gathered = lax.all_to_all(stacked, "exp", 0, 0, tiled=True)
    all_max = gathered[:, 0]
    all_mass = gathered[:, 1]
    all_hit = gathered[:, 2]
    final_max = jnp.max(all_max, axis=0)
    final_mass = jnp.sum(all_mass * jnp.exp(all_max - final_max[None]), axis=0)
    final_hit = jnp.sum(all_hit, axis=0)
    token_logp = final_hit - (final_max + jnp.log(final_mass))
    difference = token_logp[0] - token_logp[1]
    seq_sums = jnp.sum(member.astype(jnp.float32) * difference[:, None], axis=0)
    devices = lax.axis_size("req") * lax.axis_size("exp")
    per_device_seqs = seq_sums.shape[0]
    everyone = devices * per_device_seqs
    dense_totals = jnp.sum(
        (owners[:, None] == jnp.arange(everyone, dtype=jnp.int32)[None, :]).astype(jnp.float32)
        * seq_sums[:, None],
        axis=0,
    )
    delivered = lax.all_to_all(
        dense_totals.reshape(devices, per_device_seqs), ("req", "exp"), 0, 0, tiled=True
    )
    seq_totals = jnp.sum(delivered, axis=0)
    return (token_logp, seq_totals)


def solution(mesh):
    in_specs = (
        P(None, ("req", "exp"), None),
        P(("req", "exp"), None),
        P("req"),
        P(None, ("req", "exp"), None),
        P(None, ("req", "exp"), None),
        P(("req", "exp")),
        P(),
        P(),
        P(),
        P(None, "exp", None, None),
        P(None, "exp", None, None),
        P(None, "exp", None),
    )
    out_specs = (P(None, ("req", "exp")), P(("req", "exp")))
    return jax.shard_map(
        per_device, mesh=mesh, in_specs=in_specs, out_specs=out_specs, check_vma=False
    )
```

```python
import jax
import jax.numpy as jnp
from jax import lax
from jax.sharding import PartitionSpec as P

HEADS = 16
KV_HEADS = 8
HEAD_DIM = 64
EXPERT_FF = 512
EXPERTS = 32
TOP = 8
CAP = 40


EPSILON = 1e-06
RESIDUAL_SCALE = 0.22
SCORE_SCALE = 0.015625
LOGIT_DIVISOR = 6.0
ROTARY_BASE = 10000.0


def combined_all(x, axis, combine):
    everything = jax.tree.map(lambda part: lax.all_gather(part, axis), x)
    initial = jax.tree.map(lambda part: part[0], everything)

    def step(k, so_far):
        return combine(so_far, jax.tree.map(lambda part: part[k], everything))

    return lax.fori_loop(1, lax.axis_size(axis), step, initial)


def root_norm(values, gain_row):
    values = values.astype(jnp.float32)
    scaled = lax.rsqrt(jnp.mean(values * values, axis=-1, keepdims=True) + EPSILON)
    return values * scaled * gain_row


def segment_table(length_row, token_count):
    seq_ends = jnp.cumsum(length_row)
    seq_starts = seq_ends - length_row
    places = jnp.arange(token_count, dtype=jnp.int32)
    segment = jnp.sum((places[:, None] >= seq_ends[None, :]).astype(jnp.int32), axis=1)
    member = segment[:, None] == jnp.arange(length_row.shape[0], dtype=jnp.int32)[None, :]
    position = places - jnp.sum(member.astype(jnp.int32) * seq_starts[None, :], axis=1)
    return (segment, member, position)


def rotary(values, position):
    half_dim = values.shape[-1] // 2
    frequency = ROTARY_BASE ** (-2.0 * jnp.arange(half_dim, dtype=jnp.float32) / values.shape[-1])
    angles = position.astype(jnp.float32)[:, None] * frequency[None, :]
    angles = jnp.concatenate([angles, angles], axis=-1)[:, None, :]
    leading = values[..., :half_dim]
    trailing = values[..., half_dim:]
    turned = jnp.concatenate([-trailing, leading], axis=-1)
    return values * jnp.cos(angles) + turned * jnp.sin(angles)


def attend(block_states, segment, position, gain_row, qkv_weight, out_weight):
    token_count = block_states.shape[0]
    group_size = HEADS // KV_HEADS
    normed = root_norm(block_states, gain_row).astype(jnp.bfloat16)
    mixed = jnp.dot(normed, qkv_weight, preferred_element_type=jnp.float32)
    queries = rotary(
        mixed[:, : HEADS * HEAD_DIM].reshape(token_count, HEADS, HEAD_DIM), position
    ).astype(jnp.bfloat16)
    keys_all = rotary(
        mixed[:, HEADS * HEAD_DIM : (HEADS + KV_HEADS) * HEAD_DIM].reshape(
            token_count, KV_HEADS, HEAD_DIM
        ),
        position,
    ).astype(jnp.bfloat16)
    values_all = (
        mixed[:, (HEADS + KV_HEADS) * HEAD_DIM :]
        .reshape(token_count, KV_HEADS, HEAD_DIM)
        .astype(jnp.bfloat16)
    )
    grouped = queries.reshape(token_count, KV_HEADS, group_size, HEAD_DIM)
    scores = (
        jnp.einsum("tgqd,sgd->gqts", grouped, keys_all, preferred_element_type=jnp.float32)
        * SCORE_SCALE
    )
    places = jnp.arange(token_count, dtype=jnp.int32)
    allowed = (segment[:, None] == segment[None, :]) & (places[None, :] <= places[:, None])
    scores = jnp.where(allowed, scores, -1e30)
    highest = jnp.max(scores, axis=-1, keepdims=True)
    weights = jnp.exp(scores - highest)
    weights = (weights / jnp.sum(weights, axis=-1, keepdims=True)).astype(jnp.bfloat16)
    attended = jnp.einsum(
        "gqts,sgd->tgqd", weights, values_all, preferred_element_type=jnp.float32
    ).astype(jnp.bfloat16)
    projected = jnp.dot(
        attended.reshape(token_count, HEADS * HEAD_DIM),
        out_weight,
        preferred_element_type=jnp.float32,
    )
    summed = block_states.astype(jnp.float32) + RESIDUAL_SCALE * projected
    return lax.reduce_precision(summed, exponent_bits=8, mantissa_bits=7).astype(jnp.bfloat16)


def join_parts(first_part, second_part):
    first_max, first_mass, first_hit = first_part
    second_max, second_mass, second_hit = second_part
    joined_max = jnp.maximum(first_max, second_max)
    joined_mass = first_mass * jnp.exp(first_max - joined_max) + second_mass * jnp.exp(
        second_max - joined_max
    )
    return (joined_max, joined_mass, first_hit + second_hit)


def per_device(
    states,
    lengths,
    targets,
    routes,
    gate_probs,
    owners,
    norm_gains,
    qkv_weight,
    out_weight,
    expert_in,
    expert_down,
    vocab_head,
):
    token_count = states.shape[1]
    width = states.shape[2]
    segment, member, position = segment_table(lengths[0], token_count)
    groups = lax.axis_size("chip") * lax.axis_size("core")
    local_count = expert_in.shape[1]
    pairs = token_count * TOP
    slots = EXPERTS * CAP
    pair_ids = jnp.arange(pairs, dtype=jnp.int32)
    lower = (pair_ids[None, :] <= pair_ids[:, None]).astype(jnp.bfloat16)
    slot_ids = jnp.arange(slots, dtype=jnp.int32)
    chip = lax.axis_index("chip")
    core = lax.axis_index("core")
    chips = lax.axis_size("chip")
    vocab_rows = vocab_head.shape[1]
    own_shard = chip * 2 + core
    other_shard = chip * 2 + (1 - core)
    partner_head = lax.ppermute(vocab_head, "core", perm=[(0, 1), (1, 0)])
    pair_rows = 2 * vocab_rows
    vocab_ids = jnp.arange(pair_rows, dtype=jnp.int32)
    mine = jnp.take(targets.reshape(chips, 2, token_count), core, axis=1).reshape(chips * token_count)
    place_in = mine % vocab_rows
    wanted_all = jnp.where(
        mine // vocab_rows == own_shard,
        place_in,
        jnp.where(mine // vocab_rows == other_shard, place_in + vocab_rows, -1),
    )
    block_rows = 1024

    def model_entry(which):
        residual = attend(
            states[which],
            segment,
            position,
            norm_gains[which, 0],
            qkv_weight[which],
            out_weight[which],
        )
        moe_in = root_norm(residual, norm_gains[which, 1]).astype(jnp.bfloat16)
        flat_routes = routes[which].reshape(pairs)
        onehot = (flat_routes[:, None] == jnp.arange(EXPERTS, dtype=jnp.int32)).astype(
            jnp.bfloat16
        )
        running = jnp.dot(lower, onehot, preferred_element_type=jnp.float32)
        rank_slot = jnp.sum((running - 1.0) * onehot.astype(jnp.float32), axis=1).astype(jnp.int32)
        local_slot = (flat_routes * CAP + rank_slot).reshape(token_count, TOP)
        chooser = (local_slot.reshape(pairs)[:, None] == slot_ids[None, :]).astype(jnp.bfloat16)
        repeated = jnp.repeat(moe_in, TOP, axis=0)
        outgoing = jnp.einsum(
            "ps,pd->sd", chooser, repeated, preferred_element_type=jnp.float32
        ).astype(jnp.bfloat16)
        return residual, local_slot, outgoing.reshape(groups, local_count * CAP, width)

    def model_experts(which, arrived):
        inputs = arrived.reshape(groups, local_count, CAP, width)
        gate_up = jnp.einsum(
            "slcd,ldf->slcf", inputs, expert_in[which], preferred_element_type=jnp.float32
        )
        hidden = (jax.nn.silu(gate_up[..., :EXPERT_FF]) * gate_up[..., EXPERT_FF:]).astype(
            jnp.bfloat16
        )
        produced = jnp.einsum(
            "slcf,lfd->slcd", hidden, expert_down[which], preferred_element_type=jnp.float32
        ).astype(jnp.bfloat16)
        return produced.reshape(groups, local_count * CAP, width)

    def model_exit(which, residual, local_slot, returned):
        returned = returned.reshape(slots, width)
        picker = (local_slot[..., None] == slot_ids[None, None, :]).astype(jnp.bfloat16)
        picked = jnp.einsum("tks,sd->tkd", picker, returned, preferred_element_type=jnp.float32)
        mixture = jnp.sum(gate_probs[which][..., None] * picked, axis=1)
        final = root_norm(
            residual.astype(jnp.float32) + RESIDUAL_SCALE * mixture, norm_gains[which, 2]
        ).astype(jnp.bfloat16)
        return final

    def model_stats(which, chunk):
        chunk_rows = chunk.shape[0]
        block_count = chunk_rows // block_rows
        head = jnp.concatenate([vocab_head[which], partner_head[which]], axis=0)

        def one_block(block_number):
            row_block = lax.dynamic_slice_in_dim(chunk, block_number * block_rows, block_rows, 0)
            wanted = lax.dynamic_slice_in_dim(wanted_all, block_number * block_rows, block_rows, 0)
            logits = (
                jnp.einsum("td,vd->tv", row_block, head, preferred_element_type=jnp.float32)
                / LOGIT_DIVISOR
            )
            highest = jnp.max(logits, axis=1)
            masses = jnp.sum(jnp.exp(logits - highest[:, None]), axis=1)
            chosen = jnp.sum(jnp.where(wanted[:, None] == vocab_ids[None, :], logits, 0.0), axis=1)
            return jnp.stack([highest, masses, chosen])

        stats = lax.map(one_block, jnp.arange(block_count, dtype=jnp.int32))
        return jnp.transpose(stats, (1, 0, 2)).reshape(3, chips, token_count)

    def exchange(blocks):
        return lax.all_to_all(blocks, ("chip", "core"), split_axis=0, concat_axis=0, tiled=True)

    row_span = local_count * CAP
    residual_first, slot_first, outgoing_first = model_entry(0)
    produced_first = model_experts(0, exchange(outgoing_first))
    residual_second, slot_second, outgoing_second = model_entry(1)
    crossed = exchange(jnp.concatenate([produced_first, outgoing_second], axis=1))
    final_first = model_exit(0, residual_first, slot_first, crossed[:, :row_span])
    gathered_first = lax.all_gather(final_first, "chip", axis=0, tiled=True)
    produced_second = model_experts(1, crossed[:, row_span:])
    final_second = model_exit(1, residual_second, slot_second, exchange(produced_second))
    gathered_second = lax.all_gather(final_second, "chip", axis=0, tiled=True)
    stats_first = model_stats(0, gathered_first)
    stats_second = model_stats(1, gathered_second)
    stacked = jnp.transpose(jnp.stack([stats_first, stats_second]), (2, 1, 0, 3))
    gathered = lax.all_to_all(stacked, "chip", 0, 0, tiled=True)
    all_max = gathered[:, 0]
    all_mass = gathered[:, 1]
    all_hit = gathered[:, 2]
    final_max = jnp.max(all_max, axis=0)
    final_mass = jnp.sum(all_mass * jnp.exp(all_max - final_max[None]), axis=0)
    final_hit = jnp.sum(all_hit, axis=0)
    token_logp = final_hit - (final_max + jnp.log(final_mass))
    difference = token_logp[0] - token_logp[1]
    seq_sums = jnp.sum(member.astype(jnp.float32) * difference[:, None], axis=0)
    devices = lax.axis_size("req") * groups
    per_device_seqs = seq_sums.shape[0]
    everyone = devices * per_device_seqs
    dense_totals = jnp.sum(
        (owners[:, None] == jnp.arange(everyone, dtype=jnp.int32)[None, :]).astype(jnp.float32)
        * seq_sums[:, None],
        axis=0,
    )
    delivered = lax.all_to_all(
        dense_totals.reshape(devices, per_device_seqs), ("req", "chip", "core"), 0, 0, tiled=True
    )
    seq_totals = jnp.sum(delivered, axis=0)
    return (token_logp, seq_totals)


def solution(mesh):
    requests = mesh.shape["req"]
    spread = mesh.shape["exp"]
    split_mesh = jax.sharding.Mesh(
        mesh.devices.reshape(requests, spread // 2, 2), ("req", "chip", "core")
    )
    every = ("req", "chip", "core")
    group = ("chip", "core")
    in_specs = (
        P(None, every, None),
        P(every, None),
        P("req"),
        P(None, every, None),
        P(None, every, None),
        P(every),
        P(),
        P(),
        P(),
        P(None, group, None, None),
        P(None, group, None, None),
        P(None, group, None),
    )
    out_specs = (P(None, every), P(every))
    return jax.shard_map(
        per_device, mesh=split_mesh, in_specs=in_specs, out_specs=out_specs, check_vma=False
    )
```

```python
import jax
import jax.numpy as jnp
from jax import lax
from jax.sharding import PartitionSpec as P

HEADS = 16
KV_HEADS = 8
HEAD_DIM = 64
EXPERT_FF = 512
EXPERTS = 32
TOP = 8
CAP = 40


EPSILON = 1e-06
RESIDUAL_SCALE = 0.22
SCORE_SCALE = 0.015625
LOGIT_DIVISOR = 6.0
ROTARY_BASE = 10000.0


def combined_all(x, axis, combine):
    everything = jax.tree.map(lambda part: lax.all_gather(part, axis), x)
    initial = jax.tree.map(lambda part: part[0], everything)

    def step(k, so_far):
        return combine(so_far, jax.tree.map(lambda part: part[k], everything))

    return lax.fori_loop(1, lax.axis_size(axis), step, initial)


def root_norm(values, gain_row):
    values = values.astype(jnp.float32)
    scaled = lax.rsqrt(jnp.mean(values * values, axis=-1, keepdims=True) + EPSILON)
    return values * scaled * gain_row


def segment_table(length_row, token_count):
    seq_ends = jnp.cumsum(length_row)
    seq_starts = seq_ends - length_row
    places = jnp.arange(token_count, dtype=jnp.int32)
    segment = jnp.sum((places[:, None] >= seq_ends[None, :]).astype(jnp.int32), axis=1)
    member = segment[:, None] == jnp.arange(length_row.shape[0], dtype=jnp.int32)[None, :]
    position = places - jnp.sum(member.astype(jnp.int32) * seq_starts[None, :], axis=1)
    return (segment, member, position)


def rotary(values, position):
    half_dim = values.shape[-1] // 2
    frequency = ROTARY_BASE ** (-2.0 * jnp.arange(half_dim, dtype=jnp.float32) / values.shape[-1])
    angles = position.astype(jnp.float32)[:, None] * frequency[None, :]
    angles = jnp.concatenate([angles, angles], axis=-1)[:, None, :]
    leading = values[..., :half_dim]
    trailing = values[..., half_dim:]
    turned = jnp.concatenate([-trailing, leading], axis=-1)
    return values * jnp.cos(angles) + turned * jnp.sin(angles)


def attend(block_states, segment, position, gain_row, qkv_weight, out_weight):
    token_count = block_states.shape[0]
    group_size = HEADS // KV_HEADS
    normed = root_norm(block_states, gain_row).astype(jnp.bfloat16)
    mixed = jnp.dot(normed, qkv_weight, preferred_element_type=jnp.float32)
    queries = rotary(
        mixed[:, : HEADS * HEAD_DIM].reshape(token_count, HEADS, HEAD_DIM), position
    ).astype(jnp.bfloat16)
    keys_all = rotary(
        mixed[:, HEADS * HEAD_DIM : (HEADS + KV_HEADS) * HEAD_DIM].reshape(
            token_count, KV_HEADS, HEAD_DIM
        ),
        position,
    ).astype(jnp.bfloat16)
    values_all = (
        mixed[:, (HEADS + KV_HEADS) * HEAD_DIM :]
        .reshape(token_count, KV_HEADS, HEAD_DIM)
        .astype(jnp.bfloat16)
    )
    grouped = queries.reshape(token_count, KV_HEADS, group_size, HEAD_DIM)
    scores = (
        jnp.einsum("tgqd,sgd->gqts", grouped, keys_all, preferred_element_type=jnp.float32)
        * SCORE_SCALE
    )
    places = jnp.arange(token_count, dtype=jnp.int32)
    allowed = (segment[:, None] == segment[None, :]) & (places[None, :] <= places[:, None])
    scores = jnp.where(allowed, scores, -1e30)
    highest = jnp.max(scores, axis=-1, keepdims=True)
    weights = jnp.exp(scores - highest)
    weights = (weights / jnp.sum(weights, axis=-1, keepdims=True)).astype(jnp.bfloat16)
    attended = jnp.einsum(
        "gqts,sgd->tgqd", weights, values_all, preferred_element_type=jnp.float32
    ).astype(jnp.bfloat16)
    projected = jnp.dot(
        attended.reshape(token_count, HEADS * HEAD_DIM),
        out_weight,
        preferred_element_type=jnp.float32,
    )
    summed = block_states.astype(jnp.float32) + RESIDUAL_SCALE * projected
    return lax.reduce_precision(summed, exponent_bits=8, mantissa_bits=7).astype(jnp.bfloat16)


def join_parts(first_part, second_part):
    first_max, first_mass, first_hit = first_part
    second_max, second_mass, second_hit = second_part
    joined_max = jnp.maximum(first_max, second_max)
    joined_mass = first_mass * jnp.exp(first_max - joined_max) + second_mass * jnp.exp(
        second_max - joined_max
    )
    return (joined_max, joined_mass, first_hit + second_hit)


def per_device(
    states,
    lengths,
    targets,
    routes,
    gate_probs,
    owners,
    norm_gains,
    qkv_weight,
    out_weight,
    expert_in,
    expert_down,
    vocab_head,
):
    token_count = states.shape[1]
    width = states.shape[2]
    segment, member, position = segment_table(lengths[0], token_count)
    groups = lax.axis_size("chip") * lax.axis_size("core")
    local_count = expert_in.shape[1]
    pairs = token_count * TOP
    slots = EXPERTS * CAP
    pair_ids = jnp.arange(pairs, dtype=jnp.int32)
    lower = (pair_ids[None, :] <= pair_ids[:, None]).astype(jnp.bfloat16)
    slot_ids = jnp.arange(slots, dtype=jnp.int32)
    chip = lax.axis_index("chip")
    core = lax.axis_index("core")
    chips = lax.axis_size("chip")
    vocab_rows = vocab_head.shape[1]
    own_shard = chip * 2 + core
    other_shard = chip * 2 + (1 - core)
    partner_head = lax.ppermute(vocab_head, "core", perm=[(0, 1), (1, 0)])
    vocab_ids = jnp.arange(vocab_rows, dtype=jnp.int32)
    mine = jnp.take(targets.reshape(chips, 2, token_count), core, axis=1).reshape(chips * token_count)
    place_in = mine % vocab_rows
    wanted_all = jnp.where(
        mine // vocab_rows == own_shard,
        place_in,
        jnp.where(mine // vocab_rows == other_shard, place_in + vocab_rows, -1),
    )
    block_rows = 1024

    def model_entry(which):
        residual = attend(
            states[which],
            segment,
            position,
            norm_gains[which, 0],
            qkv_weight[which],
            out_weight[which],
        )
        moe_in = root_norm(residual, norm_gains[which, 1]).astype(jnp.bfloat16)
        flat_routes = routes[which].reshape(pairs)
        onehot = (flat_routes[:, None] == jnp.arange(EXPERTS, dtype=jnp.int32)).astype(
            jnp.bfloat16
        )
        running = jnp.dot(lower, onehot, preferred_element_type=jnp.float32)
        rank_slot = jnp.sum((running - 1.0) * onehot.astype(jnp.float32), axis=1).astype(jnp.int32)
        local_slot = (flat_routes * CAP + rank_slot).reshape(token_count, TOP)
        chooser = (local_slot.reshape(pairs)[:, None] == slot_ids[None, :]).astype(jnp.bfloat16)
        repeated = jnp.repeat(moe_in, TOP, axis=0)
        outgoing = jnp.einsum(
            "ps,pd->sd", chooser, repeated, preferred_element_type=jnp.float32
        ).astype(jnp.bfloat16)
        return residual, local_slot, outgoing.reshape(groups, local_count * CAP, width)

    def model_experts(which, arrived):
        inputs = arrived.reshape(groups, local_count, CAP, width)
        gate_up = jnp.einsum(
            "slcd,ldf->slcf", inputs, expert_in[which], preferred_element_type=jnp.float32
        )
        hidden = (jax.nn.silu(gate_up[..., :EXPERT_FF]) * gate_up[..., EXPERT_FF:]).astype(
            jnp.bfloat16
        )
        produced = jnp.einsum(
            "slcf,lfd->slcd", hidden, expert_down[which], preferred_element_type=jnp.float32
        ).astype(jnp.bfloat16)
        return produced.reshape(groups, local_count * CAP, width)

    def model_exit(which, residual, local_slot, returned):
        returned = returned.reshape(slots, width)
        picker = (local_slot[..., None] == slot_ids[None, None, :]).astype(jnp.bfloat16)
        picked = jnp.einsum("tks,sd->tkd", picker, returned, preferred_element_type=jnp.float32)
        mixture = jnp.sum(gate_probs[which][..., None] * picked, axis=1)
        final = root_norm(
            residual.astype(jnp.float32) + RESIDUAL_SCALE * mixture, norm_gains[which, 2]
        ).astype(jnp.bfloat16)
        return final

    def model_stats(which, chunk):
        chunk_rows = chunk.shape[0]
        block_count = chunk_rows // block_rows

        def one_block(block_number):
            row_block = lax.dynamic_slice_in_dim(chunk, block_number * block_rows, block_rows, 0)
            wanted = lax.dynamic_slice_in_dim(wanted_all, block_number * block_rows, block_rows, 0)
            near = (
                jnp.einsum(
                    "td,vd->tv", row_block, vocab_head[which], preferred_element_type=jnp.float32
                )
                / LOGIT_DIVISOR
            )
            far = (
                jnp.einsum(
                    "td,vd->tv", row_block, partner_head[which], preferred_element_type=jnp.float32
                )
                / LOGIT_DIVISOR
            )
            highest = jnp.maximum(jnp.max(near, axis=1), jnp.max(far, axis=1))
            masses = jnp.sum(jnp.exp(near - highest[:, None]), axis=1) + jnp.sum(
                jnp.exp(far - highest[:, None]), axis=1
            )
            chosen = jnp.sum(
                jnp.where(wanted[:, None] == vocab_ids[None, :], near, 0.0), axis=1
            ) + jnp.sum(jnp.where(wanted[:, None] == vocab_ids[None, :] + vocab_rows, far, 0.0), axis=1)
            return jnp.stack([highest, masses, chosen])

        stats = lax.map(one_block, jnp.arange(block_count, dtype=jnp.int32))
        return jnp.transpose(stats, (1, 0, 2)).reshape(3, chips, token_count)

    def exchange(blocks):
        return lax.all_to_all(blocks, ("chip", "core"), split_axis=0, concat_axis=0, tiled=True)

    row_span = local_count * CAP
    residual_first, slot_first, outgoing_first = model_entry(0)
    produced_first = model_experts(0, exchange(outgoing_first))
    residual_second, slot_second, outgoing_second = model_entry(1)
    crossed = exchange(jnp.concatenate([produced_first, outgoing_second], axis=1))
    final_first = model_exit(0, residual_first, slot_first, crossed[:, :row_span])
    gathered_first = lax.all_gather(final_first, "chip", axis=0, tiled=True)
    produced_second = model_experts(1, crossed[:, row_span:])
    final_second = model_exit(1, residual_second, slot_second, exchange(produced_second))
    gathered_second = lax.all_gather(final_second, "chip", axis=0, tiled=True)
    stats_first = model_stats(0, gathered_first)
    stats_second = model_stats(1, gathered_second)
    stacked = jnp.transpose(jnp.stack([stats_first, stats_second]), (2, 1, 0, 3))
    gathered = lax.all_to_all(stacked, "chip", 0, 0, tiled=True)
    all_max = gathered[:, 0]
    all_mass = gathered[:, 1]
    all_hit = gathered[:, 2]
    final_max = jnp.max(all_max, axis=0)
    final_mass = jnp.sum(all_mass * jnp.exp(all_max - final_max[None]), axis=0)
    final_hit = jnp.sum(all_hit, axis=0)
    token_logp = final_hit - (final_max + jnp.log(final_mass))
    difference = token_logp[0] - token_logp[1]
    seq_sums = jnp.sum(member.astype(jnp.float32) * difference[:, None], axis=0)
    devices = lax.axis_size("req") * groups
    per_device_seqs = seq_sums.shape[0]
    everyone = devices * per_device_seqs
    dense_totals = jnp.sum(
        (owners[:, None] == jnp.arange(everyone, dtype=jnp.int32)[None, :]).astype(jnp.float32)
        * seq_sums[:, None],
        axis=0,
    )
    delivered = lax.all_to_all(
        dense_totals.reshape(devices, per_device_seqs), ("req", "chip", "core"), 0, 0, tiled=True
    )
    seq_totals = jnp.sum(delivered, axis=0)
    return (token_logp, seq_totals)


def solution(mesh):
    requests = mesh.shape["req"]
    spread = mesh.shape["exp"]
    split_mesh = jax.sharding.Mesh(
        mesh.devices.reshape(requests, spread // 2, 2), ("req", "chip", "core")
    )
    every = ("req", "chip", "core")
    group = ("chip", "core")
    in_specs = (
        P(None, every, None),
        P(every, None),
        P("req"),
        P(None, every, None),
        P(None, every, None),
        P(every),
        P(),
        P(),
        P(),
        P(None, group, None, None),
        P(None, group, None, None),
        P(None, group, None),
    )
    out_specs = (P(None, every), P(every))
    return jax.shard_map(
        per_device, mesh=split_mesh, in_specs=in_specs, out_specs=out_specs, check_vma=False
    )
```

```python
import jax
import jax.numpy as jnp
from jax import lax
from jax.sharding import PartitionSpec as P

HEADS = 16
KV_HEADS = 8
HEAD_DIM = 64
EXPERT_FF = 512
EXPERTS = 32
TOP = 8
CAP = 40


EPSILON = 1e-06
RESIDUAL_SCALE = 0.22
SCORE_SCALE = 0.015625
LOGIT_DIVISOR = 6.0
ROTARY_BASE = 10000.0


def combined_all(x, axis, combine):
    everything = jax.tree.map(lambda part: lax.all_gather(part, axis), x)
    initial = jax.tree.map(lambda part: part[0], everything)

    def step(k, so_far):
        return combine(so_far, jax.tree.map(lambda part: part[k], everything))

    return lax.fori_loop(1, lax.axis_size(axis), step, initial)


def root_norm(values, gain_row):
    values = values.astype(jnp.float32)
    scaled = lax.rsqrt(jnp.mean(values * values, axis=-1, keepdims=True) + EPSILON)
    return values * scaled * gain_row


def segment_table(length_row, token_count):
    seq_ends = jnp.cumsum(length_row)
    seq_starts = seq_ends - length_row
    places = jnp.arange(token_count, dtype=jnp.int32)
    segment = jnp.sum((places[:, None] >= seq_ends[None, :]).astype(jnp.int32), axis=1)
    member = segment[:, None] == jnp.arange(length_row.shape[0], dtype=jnp.int32)[None, :]
    position = places - jnp.sum(member.astype(jnp.int32) * seq_starts[None, :], axis=1)
    return (segment, member, position)


def rotary(values, position):
    half_dim = values.shape[-1] // 2
    frequency = ROTARY_BASE ** (-2.0 * jnp.arange(half_dim, dtype=jnp.float32) / values.shape[-1])
    angles = position.astype(jnp.float32)[:, None] * frequency[None, :]
    angles = jnp.concatenate([angles, angles], axis=-1)[:, None, :]
    leading = values[..., :half_dim]
    trailing = values[..., half_dim:]
    turned = jnp.concatenate([-trailing, leading], axis=-1)
    return values * jnp.cos(angles) + turned * jnp.sin(angles)


def attend(block_states, segment, position, gain_row, qkv_weight, out_weight):
    token_count = block_states.shape[0]
    group_size = HEADS // KV_HEADS
    normed = root_norm(block_states, gain_row).astype(jnp.bfloat16)
    mixed = jnp.dot(normed, qkv_weight, preferred_element_type=jnp.float32)
    queries = rotary(
        mixed[:, : HEADS * HEAD_DIM].reshape(token_count, HEADS, HEAD_DIM), position
    ).astype(jnp.bfloat16)
    keys_all = rotary(
        mixed[:, HEADS * HEAD_DIM : (HEADS + KV_HEADS) * HEAD_DIM].reshape(
            token_count, KV_HEADS, HEAD_DIM
        ),
        position,
    ).astype(jnp.bfloat16)
    values_all = (
        mixed[:, (HEADS + KV_HEADS) * HEAD_DIM :]
        .reshape(token_count, KV_HEADS, HEAD_DIM)
        .astype(jnp.bfloat16)
    )
    grouped = queries.reshape(token_count, KV_HEADS, group_size, HEAD_DIM)
    scores = (
        jnp.einsum("tgqd,sgd->gqts", grouped, keys_all, preferred_element_type=jnp.float32)
        * SCORE_SCALE
    )
    places = jnp.arange(token_count, dtype=jnp.int32)
    allowed = (segment[:, None] == segment[None, :]) & (places[None, :] <= places[:, None])
    scores = jnp.where(allowed, scores, -1e30)
    highest = jnp.max(scores, axis=-1, keepdims=True)
    weights = jnp.exp(scores - highest)
    weights = (weights / jnp.sum(weights, axis=-1, keepdims=True)).astype(jnp.bfloat16)
    attended = jnp.einsum(
        "gqts,sgd->tgqd", weights, values_all, preferred_element_type=jnp.float32
    ).astype(jnp.bfloat16)
    projected = jnp.dot(
        attended.reshape(token_count, HEADS * HEAD_DIM),
        out_weight,
        preferred_element_type=jnp.float32,
    )
    summed = block_states.astype(jnp.float32) + RESIDUAL_SCALE * projected
    return lax.reduce_precision(summed, exponent_bits=8, mantissa_bits=7).astype(jnp.bfloat16)


def join_parts(first_part, second_part):
    first_max, first_mass, first_hit = first_part
    second_max, second_mass, second_hit = second_part
    joined_max = jnp.maximum(first_max, second_max)
    joined_mass = first_mass * jnp.exp(first_max - joined_max) + second_mass * jnp.exp(
        second_max - joined_max
    )
    return (joined_max, joined_mass, first_hit + second_hit)


def per_device(
    states,
    lengths,
    targets,
    routes,
    gate_probs,
    owners,
    norm_gains,
    qkv_weight,
    out_weight,
    expert_in,
    expert_down,
    vocab_head,
):
    token_count = states.shape[1]
    width = states.shape[2]
    segment, member, position = segment_table(lengths[0], token_count)
    groups = lax.axis_size("exp")
    local_count = expert_in.shape[1]
    pairs = token_count * TOP
    slots = EXPERTS * CAP
    pair_ids = jnp.arange(pairs, dtype=jnp.int32)
    lower = (pair_ids[None, :] <= pair_ids[:, None]).astype(jnp.bfloat16)
    slot_ids = jnp.arange(slots, dtype=jnp.int32)
    shard = lax.axis_index("exp")
    vocab_rows = vocab_head.shape[1]
    lowest = shard * vocab_rows
    vocab_ids = jnp.arange(vocab_rows, dtype=jnp.int32)
    wanted_all = targets - lowest
    block_rows = 2048

    def model_entry(which):
        residual = attend(
            states[which],
            segment,
            position,
            norm_gains[which, 0],
            qkv_weight[which],
            out_weight[which],
        )
        moe_in = root_norm(residual, norm_gains[which, 1]).astype(jnp.bfloat16)
        flat_routes = routes[which].reshape(pairs)
        onehot = (flat_routes[:, None] == jnp.arange(EXPERTS, dtype=jnp.int32)).astype(
            jnp.bfloat16
        )
        running = jnp.dot(lower, onehot, preferred_element_type=jnp.float32)
        rank_slot = jnp.sum((running - 1.0) * onehot.astype(jnp.float32), axis=1).astype(jnp.int32)
        local_slot = (flat_routes * CAP + rank_slot).reshape(token_count, TOP)
        chooser = (local_slot.reshape(pairs)[:, None] == slot_ids[None, :]).astype(jnp.bfloat16)
        repeated = jnp.repeat(moe_in, TOP, axis=0)
        outgoing = jnp.einsum(
            "ps,pd->sd", chooser, repeated, preferred_element_type=jnp.float32
        ).astype(jnp.bfloat16)
        return residual, local_slot, outgoing.reshape(groups, local_count * CAP, width)

    def model_experts(which, arrived):
        inputs = arrived.reshape(groups, local_count, CAP, width)
        gate_up = jnp.einsum(
            "slcd,ldf->slcf", inputs, expert_in[which], preferred_element_type=jnp.float32
        )
        hidden = (jax.nn.silu(gate_up[..., :EXPERT_FF]) * gate_up[..., EXPERT_FF:]).astype(
            jnp.bfloat16
        )
        produced = jnp.einsum(
            "slcf,lfd->slcd", hidden, expert_down[which], preferred_element_type=jnp.float32
        ).astype(jnp.bfloat16)
        return produced.reshape(groups, local_count * CAP, width)

    def model_exit(which, residual, local_slot, returned):
        returned = returned.reshape(slots, width)
        blend = jnp.sum(
            jnp.where(
                local_slot[..., None] == slot_ids[None, None, :], gate_probs[which][..., None], 0.0
            ),
            axis=1,
        )
        blend_high = blend.astype(jnp.bfloat16)
        blend_low = (blend - blend_high.astype(jnp.float32)).astype(jnp.bfloat16)
        mixture = jnp.dot(blend_high, returned, preferred_element_type=jnp.float32) + jnp.dot(
            blend_low, returned, preferred_element_type=jnp.float32
        )
        final = root_norm(
            residual.astype(jnp.float32) + RESIDUAL_SCALE * mixture, norm_gains[which, 2]
        ).astype(jnp.bfloat16)
        return final

    def exchange(blocks):
        return lax.all_to_all(blocks, "exp", split_axis=0, concat_axis=0, tiled=True)

    def model_stats(which, chunk):
        chunk_rows = chunk.shape[0]
        block_count = chunk_rows // block_rows
        def one_block(block_number):
            head = vocab_head[which]
            row_block = lax.dynamic_slice_in_dim(chunk, block_number * block_rows, block_rows, 0)
            wanted = lax.dynamic_slice_in_dim(wanted_all, block_number * block_rows, block_rows, 0)
            logits = (
                jnp.einsum("td,vd->tv", row_block, head, preferred_element_type=jnp.float32)
                / LOGIT_DIVISOR
            )
            highest = jnp.max(logits, axis=1)
            masses = jnp.sum(jnp.exp(logits - highest[:, None]), axis=1)
            chosen = jnp.sum(jnp.where(wanted[:, None] == vocab_ids[None, :], logits, 0.0), axis=1)
            return jnp.stack([highest, masses, chosen])

        stats = lax.map(one_block, jnp.arange(block_count, dtype=jnp.int32))
        return jnp.transpose(stats, (1, 0, 2)).reshape(3, groups, token_count)

    row_span = local_count * CAP
    residual_first, slot_first, outgoing_first = model_entry(0)
    produced_first = model_experts(0, exchange(outgoing_first))
    residual_second, slot_second, outgoing_second = model_entry(1)
    crossed = exchange(jnp.concatenate([produced_first, outgoing_second], axis=1))
    final_first = model_exit(0, residual_first, slot_first, crossed[:, :row_span])
    gathered_first = lax.all_gather(final_first, "exp", axis=0, tiled=True)
    produced_second = model_experts(1, crossed[:, row_span:])
    final_second = model_exit(1, residual_second, slot_second, exchange(produced_second))
    gathered_second = lax.all_gather(final_second, "exp", axis=0, tiled=True)
    stats_first = model_stats(0, gathered_first)
    stats_second = model_stats(1, gathered_second)
    stacked = jnp.transpose(jnp.stack([stats_first, stats_second]), (2, 1, 0, 3))
    gathered = lax.all_to_all(stacked, "exp", 0, 0, tiled=True)
    all_max = gathered[:, 0]
    all_mass = gathered[:, 1]
    all_hit = gathered[:, 2]
    final_max = jnp.max(all_max, axis=0)
    final_mass = jnp.sum(all_mass * jnp.exp(all_max - final_max[None]), axis=0)
    final_hit = jnp.sum(all_hit, axis=0)
    token_logp = final_hit - (final_max + jnp.log(final_mass))
    difference = token_logp[0] - token_logp[1]
    seq_sums = jnp.sum(member.astype(jnp.float32) * difference[:, None], axis=0)
    devices = lax.axis_size("req") * lax.axis_size("exp")
    per_device_seqs = seq_sums.shape[0]
    everyone = devices * per_device_seqs
    dense_totals = jnp.sum(
        (owners[:, None] == jnp.arange(everyone, dtype=jnp.int32)[None, :]).astype(jnp.float32)
        * seq_sums[:, None],
        axis=0,
    )
    delivered = lax.all_to_all(
        dense_totals.reshape(devices, per_device_seqs), ("req", "exp"), 0, 0, tiled=True
    )
    seq_totals = jnp.sum(delivered, axis=0)
    return (token_logp, seq_totals)


def solution(mesh):
    in_specs = (
        P(None, ("req", "exp"), None),
        P(("req", "exp"), None),
        P("req"),
        P(None, ("req", "exp"), None),
        P(None, ("req", "exp"), None),
        P(("req", "exp")),
        P(),
        P(),
        P(),
        P(None, "exp", None, None),
        P(None, "exp", None, None),
        P(None, "exp", None),
    )
    out_specs = (P(None, ("req", "exp")), P(("req", "exp")))
    return jax.shard_map(
        per_device, mesh=mesh, in_specs=in_specs, out_specs=out_specs, check_vma=False
    )
```

```python
import jax
import jax.numpy as jnp
from jax import lax
from jax.sharding import PartitionSpec as P

HEADS = 16
KV_HEADS = 8
HEAD_DIM = 64
EXPERT_FF = 512
EXPERTS = 32
TOP = 8
CAP = 40


EPSILON = 1e-06
RESIDUAL_SCALE = 0.22
SCORE_SCALE = 0.015625
LOGIT_DIVISOR = 6.0
ROTARY_BASE = 10000.0


def combined_all(x, axis, combine):
    everything = jax.tree.map(lambda part: lax.all_gather(part, axis), x)
    initial = jax.tree.map(lambda part: part[0], everything)

    def step(k, so_far):
        return combine(so_far, jax.tree.map(lambda part: part[k], everything))

    return lax.fori_loop(1, lax.axis_size(axis), step, initial)


def root_norm(values, gain_row):
    values = values.astype(jnp.float32)
    scaled = lax.rsqrt(jnp.mean(values * values, axis=-1, keepdims=True) + EPSILON)
    return values * scaled * gain_row


def segment_table(length_row, token_count):
    seq_ends = jnp.cumsum(length_row)
    seq_starts = seq_ends - length_row
    places = jnp.arange(token_count, dtype=jnp.int32)
    segment = jnp.sum((places[:, None] >= seq_ends[None, :]).astype(jnp.int32), axis=1)
    member = segment[:, None] == jnp.arange(length_row.shape[0], dtype=jnp.int32)[None, :]
    position = places - jnp.sum(member.astype(jnp.int32) * seq_starts[None, :], axis=1)
    return (segment, member, position)


def rotary(values, position):
    half_dim = values.shape[-1] // 2
    frequency = ROTARY_BASE ** (-2.0 * jnp.arange(half_dim, dtype=jnp.float32) / values.shape[-1])
    angles = position.astype(jnp.float32)[:, None] * frequency[None, :]
    angles = jnp.concatenate([angles, angles], axis=-1)[:, None, :]
    leading = values[..., :half_dim]
    trailing = values[..., half_dim:]
    turned = jnp.concatenate([-trailing, leading], axis=-1)
    return values * jnp.cos(angles) + turned * jnp.sin(angles)


def attend(block_states, segment, position, gain_row, qkv_weight, out_weight):
    token_count = block_states.shape[0]
    group_size = HEADS // KV_HEADS
    normed = root_norm(block_states, gain_row).astype(jnp.bfloat16)
    mixed = jnp.dot(normed, qkv_weight, preferred_element_type=jnp.float32)
    queries = rotary(
        mixed[:, : HEADS * HEAD_DIM].reshape(token_count, HEADS, HEAD_DIM), position
    ).astype(jnp.bfloat16)
    keys_all = rotary(
        mixed[:, HEADS * HEAD_DIM : (HEADS + KV_HEADS) * HEAD_DIM].reshape(
            token_count, KV_HEADS, HEAD_DIM
        ),
        position,
    ).astype(jnp.bfloat16)
    values_all = (
        mixed[:, (HEADS + KV_HEADS) * HEAD_DIM :]
        .reshape(token_count, KV_HEADS, HEAD_DIM)
        .astype(jnp.bfloat16)
    )
    grouped = queries.reshape(token_count, KV_HEADS, group_size, HEAD_DIM)
    scores = (
        jnp.einsum("tgqd,sgd->gqts", grouped, keys_all, preferred_element_type=jnp.float32)
        * SCORE_SCALE
    )
    places = jnp.arange(token_count, dtype=jnp.int32)
    allowed = (segment[:, None] == segment[None, :]) & (places[None, :] <= places[:, None])
    scores = jnp.where(allowed, scores, -1e30)
    highest = jnp.max(scores, axis=-1, keepdims=True)
    weights = jnp.exp(scores - highest)
    weights = (weights / jnp.sum(weights, axis=-1, keepdims=True)).astype(jnp.bfloat16)
    attended = jnp.einsum(
        "gqts,sgd->tgqd", weights, values_all, preferred_element_type=jnp.float32
    ).astype(jnp.bfloat16)
    projected = jnp.dot(
        attended.reshape(token_count, HEADS * HEAD_DIM),
        out_weight,
        preferred_element_type=jnp.float32,
    )
    summed = block_states.astype(jnp.float32) + RESIDUAL_SCALE * projected
    return lax.reduce_precision(summed, exponent_bits=8, mantissa_bits=7).astype(jnp.bfloat16)


def join_parts(first_part, second_part):
    first_max, first_mass, first_hit = first_part
    second_max, second_mass, second_hit = second_part
    joined_max = jnp.maximum(first_max, second_max)
    joined_mass = first_mass * jnp.exp(first_max - joined_max) + second_mass * jnp.exp(
        second_max - joined_max
    )
    return (joined_max, joined_mass, first_hit + second_hit)


def per_device(
    states,
    lengths,
    targets,
    routes,
    gate_probs,
    owners,
    norm_gains,
    qkv_weight,
    out_weight,
    expert_in,
    expert_down,
    vocab_head,
):
    token_count = states.shape[1]
    width = states.shape[2]
    segment, member, position = segment_table(lengths[0], token_count)
    groups = lax.axis_size("exp")
    local_count = expert_in.shape[1]
    pairs = token_count * TOP
    slots = EXPERTS * CAP
    pair_ids = jnp.arange(pairs, dtype=jnp.int32)
    lower = (pair_ids[None, :] <= pair_ids[:, None]).astype(jnp.bfloat16)
    slot_ids = jnp.arange(slots, dtype=jnp.int32)
    shard = lax.axis_index("exp")
    vocab_rows = vocab_head.shape[1]
    lowest = shard * vocab_rows
    vocab_ids = jnp.arange(vocab_rows, dtype=jnp.int32)
    wanted_all = targets - lowest
    block_rows = 2048

    def model_entry(which):
        residual = attend(
            states[which],
            segment,
            position,
            norm_gains[which, 0],
            qkv_weight[which],
            out_weight[which],
        )
        moe_in = root_norm(residual, norm_gains[which, 1]).astype(jnp.bfloat16)
        flat_routes = routes[which].reshape(pairs)
        onehot = (flat_routes[:, None] == jnp.arange(EXPERTS, dtype=jnp.int32)).astype(
            jnp.bfloat16
        )
        running = jnp.dot(lower, onehot, preferred_element_type=jnp.float32)
        rank_slot = jnp.sum((running - 1.0) * onehot.astype(jnp.float32), axis=1).astype(jnp.int32)
        local_slot = (flat_routes * CAP + rank_slot).reshape(token_count, TOP)
        chooser = (local_slot.reshape(pairs)[:, None] == slot_ids[None, :]).astype(jnp.bfloat16)
        owner = (pair_ids[:, None] // TOP == jnp.arange(token_count, dtype=jnp.int32)[None, :]).astype(
            jnp.bfloat16
        )
        slot_token = jnp.einsum(
            "ps,pt->st", chooser, owner, preferred_element_type=jnp.float32
        ).astype(jnp.bfloat16)
        outgoing = jnp.dot(slot_token, moe_in, preferred_element_type=jnp.float32).astype(
            jnp.bfloat16
        )
        return residual, local_slot, outgoing.reshape(groups, local_count * CAP, width)

    def model_experts(which, arrived):
        inputs = arrived.reshape(groups, local_count, CAP, width)
        gate_up = jnp.einsum(
            "slcd,ldf->slcf", inputs, expert_in[which], preferred_element_type=jnp.float32
        )
        hidden = (jax.nn.silu(gate_up[..., :EXPERT_FF]) * gate_up[..., EXPERT_FF:]).astype(
            jnp.bfloat16
        )
        produced = jnp.einsum(
            "slcf,lfd->slcd", hidden, expert_down[which], preferred_element_type=jnp.float32
        ).astype(jnp.bfloat16)
        return produced.reshape(groups, local_count * CAP, width)

    def model_exit(which, residual, local_slot, returned):
        returned = returned.reshape(slots, width)
        blend = jnp.sum(
            jnp.where(
                local_slot[..., None] == slot_ids[None, None, :], gate_probs[which][..., None], 0.0
            ),
            axis=1,
        )
        blend_high = blend.astype(jnp.bfloat16)
        blend_low = (blend - blend_high.astype(jnp.float32)).astype(jnp.bfloat16)
        mixture = jnp.dot(blend_high, returned, preferred_element_type=jnp.float32) + jnp.dot(
            blend_low, returned, preferred_element_type=jnp.float32
        )
        final = root_norm(
            residual.astype(jnp.float32) + RESIDUAL_SCALE * mixture, norm_gains[which, 2]
        ).astype(jnp.bfloat16)
        return final

    def exchange(blocks):
        return lax.all_to_all(blocks, "exp", split_axis=0, concat_axis=0, tiled=True)

    def model_stats(which, chunk):
        chunk_rows = chunk.shape[0]
        block_count = chunk_rows // block_rows
        def one_block(block_number):
            head = vocab_head[which]
            row_block = lax.dynamic_slice_in_dim(chunk, block_number * block_rows, block_rows, 0)
            wanted = lax.dynamic_slice_in_dim(wanted_all, block_number * block_rows, block_rows, 0)
            logits = (
                jnp.einsum("td,vd->tv", row_block, head, preferred_element_type=jnp.float32)
                / LOGIT_DIVISOR
            )
            highest = jnp.max(logits, axis=1)
            masses = jnp.sum(jnp.exp(logits - highest[:, None]), axis=1)
            chosen = jnp.sum(jnp.where(wanted[:, None] == vocab_ids[None, :], logits, 0.0), axis=1)
            return jnp.stack([highest, masses, chosen])

        stats = lax.map(one_block, jnp.arange(block_count, dtype=jnp.int32))
        return jnp.transpose(stats, (1, 0, 2)).reshape(3, groups, token_count)

    row_span = local_count * CAP
    residual_first, slot_first, outgoing_first = model_entry(0)
    produced_first = model_experts(0, exchange(outgoing_first))
    residual_second, slot_second, outgoing_second = model_entry(1)
    crossed = exchange(jnp.concatenate([produced_first, outgoing_second], axis=1))
    final_first = model_exit(0, residual_first, slot_first, crossed[:, :row_span])
    gathered_first = lax.all_gather(final_first, "exp", axis=0, tiled=True)
    produced_second = model_experts(1, crossed[:, row_span:])
    final_second = model_exit(1, residual_second, slot_second, exchange(produced_second))
    gathered_second = lax.all_gather(final_second, "exp", axis=0, tiled=True)
    stats_first = model_stats(0, gathered_first)
    stats_second = model_stats(1, gathered_second)
    stacked = jnp.transpose(jnp.stack([stats_first, stats_second]), (2, 1, 0, 3))
    gathered = lax.all_to_all(stacked, "exp", 0, 0, tiled=True)
    all_max = gathered[:, 0]
    all_mass = gathered[:, 1]
    all_hit = gathered[:, 2]
    final_max = jnp.max(all_max, axis=0)
    final_mass = jnp.sum(all_mass * jnp.exp(all_max - final_max[None]), axis=0)
    final_hit = jnp.sum(all_hit, axis=0)
    token_logp = final_hit - (final_max + jnp.log(final_mass))
    difference = token_logp[0] - token_logp[1]
    seq_sums = jnp.sum(member.astype(jnp.float32) * difference[:, None], axis=0)
    devices = lax.axis_size("req") * lax.axis_size("exp")
    per_device_seqs = seq_sums.shape[0]
    everyone = devices * per_device_seqs
    dense_totals = jnp.sum(
        (owners[:, None] == jnp.arange(everyone, dtype=jnp.int32)[None, :]).astype(jnp.float32)
        * seq_sums[:, None],
        axis=0,
    )
    delivered = lax.all_to_all(
        dense_totals.reshape(devices, per_device_seqs), ("req", "exp"), 0, 0, tiled=True
    )
    seq_totals = jnp.sum(delivered, axis=0)
    return (token_logp, seq_totals)


def solution(mesh):
    in_specs = (
        P(None, ("req", "exp"), None),
        P(("req", "exp"), None),
        P("req"),
        P(None, ("req", "exp"), None),
        P(None, ("req", "exp"), None),
        P(("req", "exp")),
        P(),
        P(),
        P(),
        P(None, "exp", None, None),
        P(None, "exp", None, None),
        P(None, "exp", None),
    )
    out_specs = (P(None, ("req", "exp")), P(("req", "exp")))
    return jax.shard_map(
        per_device, mesh=mesh, in_specs=in_specs, out_specs=out_specs, check_vma=False
    )
```

```python
import jax
import jax.numpy as jnp
from jax import lax
from jax.sharding import PartitionSpec as P

HEADS = 16
KV_HEADS = 8
HEAD_DIM = 64
EXPERT_FF = 512
EXPERTS = 32
TOP = 8
CAP = 40


EPSILON = 1e-06
RESIDUAL_SCALE = 0.22
SCORE_SCALE = 0.015625
LOGIT_DIVISOR = 6.0
ROTARY_BASE = 10000.0


def combined_all(x, axis, combine):
    everything = jax.tree.map(lambda part: lax.all_gather(part, axis), x)
    initial = jax.tree.map(lambda part: part[0], everything)

    def step(k, so_far):
        return combine(so_far, jax.tree.map(lambda part: part[k], everything))

    return lax.fori_loop(1, lax.axis_size(axis), step, initial)


def root_norm(values, gain_row):
    values = values.astype(jnp.float32)
    scaled = lax.rsqrt(jnp.mean(values * values, axis=-1, keepdims=True) + EPSILON)
    return values * scaled * gain_row


def segment_table(length_row, token_count):
    seq_ends = jnp.cumsum(length_row)
    seq_starts = seq_ends - length_row
    places = jnp.arange(token_count, dtype=jnp.int32)
    segment = jnp.sum((places[:, None] >= seq_ends[None, :]).astype(jnp.int32), axis=1)
    member = segment[:, None] == jnp.arange(length_row.shape[0], dtype=jnp.int32)[None, :]
    position = places - jnp.sum(member.astype(jnp.int32) * seq_starts[None, :], axis=1)
    return (segment, member, position)


def rotary(values, position):
    half_dim = values.shape[-1] // 2
    frequency = ROTARY_BASE ** (-2.0 * jnp.arange(half_dim, dtype=jnp.float32) / values.shape[-1])
    angles = position.astype(jnp.float32)[:, None] * frequency[None, :]
    angles = jnp.concatenate([angles, angles], axis=-1)[:, None, :]
    leading = values[..., :half_dim]
    trailing = values[..., half_dim:]
    turned = jnp.concatenate([-trailing, leading], axis=-1)
    return values * jnp.cos(angles) + turned * jnp.sin(angles)


def attend(block_states, segment, position, gain_row, qkv_weight, out_weight):
    token_count = block_states.shape[0]
    group_size = HEADS // KV_HEADS
    normed = root_norm(block_states, gain_row).astype(jnp.bfloat16)
    mixed = jnp.dot(normed, qkv_weight, preferred_element_type=jnp.float32)
    queries = rotary(
        mixed[:, : HEADS * HEAD_DIM].reshape(token_count, HEADS, HEAD_DIM), position
    ).astype(jnp.bfloat16)
    keys_all = rotary(
        mixed[:, HEADS * HEAD_DIM : (HEADS + KV_HEADS) * HEAD_DIM].reshape(
            token_count, KV_HEADS, HEAD_DIM
        ),
        position,
    ).astype(jnp.bfloat16)
    values_all = (
        mixed[:, (HEADS + KV_HEADS) * HEAD_DIM :]
        .reshape(token_count, KV_HEADS, HEAD_DIM)
        .astype(jnp.bfloat16)
    )
    grouped = queries.reshape(token_count, KV_HEADS, group_size, HEAD_DIM)
    scores = (
        jnp.einsum("tgqd,sgd->gqts", grouped, keys_all, preferred_element_type=jnp.float32)
        * SCORE_SCALE
    )
    places = jnp.arange(token_count, dtype=jnp.int32)
    allowed = (segment[:, None] == segment[None, :]) & (places[None, :] <= places[:, None])
    scores = jnp.where(allowed, scores, -1e30)
    highest = jnp.max(scores, axis=-1, keepdims=True)
    weights = jnp.exp(scores - highest)
    weights = (weights / jnp.sum(weights, axis=-1, keepdims=True)).astype(jnp.bfloat16)
    attended = jnp.einsum(
        "gqts,sgd->tgqd", weights, values_all, preferred_element_type=jnp.float32
    ).astype(jnp.bfloat16)
    projected = jnp.dot(
        attended.reshape(token_count, HEADS * HEAD_DIM),
        out_weight,
        preferred_element_type=jnp.float32,
    )
    summed = block_states.astype(jnp.float32) + RESIDUAL_SCALE * projected
    return lax.reduce_precision(summed, exponent_bits=8, mantissa_bits=7).astype(jnp.bfloat16)


def join_parts(first_part, second_part):
    first_max, first_mass, first_hit = first_part
    second_max, second_mass, second_hit = second_part
    joined_max = jnp.maximum(first_max, second_max)
    joined_mass = first_mass * jnp.exp(first_max - joined_max) + second_mass * jnp.exp(
        second_max - joined_max
    )
    return (joined_max, joined_mass, first_hit + second_hit)


def per_device(
    states,
    lengths,
    targets,
    routes,
    gate_probs,
    owners,
    norm_gains,
    qkv_weight,
    out_weight,
    expert_in,
    expert_down,
    vocab_head,
):
    token_count = states.shape[1]
    width = states.shape[2]
    segment, member, position = segment_table(lengths[0], token_count)
    groups = lax.axis_size("exp")
    local_count = expert_in.shape[1]
    pairs = token_count * TOP
    slots = EXPERTS * CAP
    pair_ids = jnp.arange(pairs, dtype=jnp.int32)
    lower = (pair_ids[None, :] <= pair_ids[:, None]).astype(jnp.bfloat16)
    slot_ids = jnp.arange(slots, dtype=jnp.int32)
    shard = lax.axis_index("exp")
    vocab_rows = vocab_head.shape[1]
    lowest = shard * vocab_rows
    vocab_ids = jnp.arange(vocab_rows, dtype=jnp.int32)
    wanted_all = targets - lowest
    block_rows = 2048

    def model_entry(which):
        residual = attend(
            states[which],
            segment,
            position,
            norm_gains[which, 0],
            qkv_weight[which],
            out_weight[which],
        )
        moe_in = root_norm(residual, norm_gains[which, 1]).astype(jnp.bfloat16)
        flat_routes = routes[which].reshape(pairs)
        onehot = (flat_routes[:, None] == jnp.arange(EXPERTS, dtype=jnp.int32)).astype(
            jnp.bfloat16
        )
        running = jnp.dot(lower, onehot, preferred_element_type=jnp.float32)
        rank_slot = jnp.sum((running - 1.0) * onehot.astype(jnp.float32), axis=1).astype(jnp.int32)
        local_slot = (flat_routes * CAP + rank_slot).reshape(token_count, TOP)
        chooser = (local_slot.reshape(pairs)[:, None] == slot_ids[None, :]).astype(jnp.bfloat16)
        repeated = jnp.repeat(moe_in, TOP, axis=0)
        outgoing = jnp.einsum(
            "ps,pd->sd", chooser, repeated, preferred_element_type=jnp.float32
        ).astype(jnp.bfloat16)
        return residual, local_slot, outgoing.reshape(groups, local_count * CAP, width)

    def model_experts(which, arrived):
        inputs = arrived.reshape(groups, local_count, CAP, width)
        gate_up = jnp.einsum(
            "slcd,ldf->slcf", inputs, expert_in[which], preferred_element_type=jnp.float32
        )
        hidden = (jax.nn.silu(gate_up[..., :EXPERT_FF]) * gate_up[..., EXPERT_FF:]).astype(
            jnp.bfloat16
        )
        produced = jnp.einsum(
            "slcf,lfd->slcd", hidden, expert_down[which], preferred_element_type=jnp.float32
        ).astype(jnp.bfloat16)
        return produced.reshape(groups, local_count * CAP, width)

    def model_exit(which, residual, local_slot, returned, stride=CAP):
        returned = returned.reshape(-1, width)
        row_of_slot = (local_slot // CAP) * stride + local_slot % CAP
        row_ids = jnp.arange(returned.shape[0], dtype=jnp.int32)
        blend = jnp.sum(
            jnp.where(
                row_of_slot[..., None] == row_ids[None, None, :], gate_probs[which][..., None], 0.0
            ),
            axis=1,
        )
        blend_high = blend.astype(jnp.bfloat16)
        blend_low = (blend - blend_high.astype(jnp.float32)).astype(jnp.bfloat16)
        mixture = jnp.dot(blend_high, returned, preferred_element_type=jnp.float32) + jnp.dot(
            blend_low, returned, preferred_element_type=jnp.float32
        )
        final = root_norm(
            residual.astype(jnp.float32) + RESIDUAL_SCALE * mixture, norm_gains[which, 2]
        ).astype(jnp.bfloat16)
        return final

    def exchange(blocks):
        return lax.all_to_all(blocks, "exp", split_axis=0, concat_axis=0, tiled=True)

    def model_stats(which, chunk):
        chunk_rows = chunk.shape[0]
        block_count = chunk_rows // block_rows
        def one_block(block_number):
            head = vocab_head[which]
            row_block = lax.dynamic_slice_in_dim(chunk, block_number * block_rows, block_rows, 0)
            wanted = lax.dynamic_slice_in_dim(wanted_all, block_number * block_rows, block_rows, 0)
            logits = (
                jnp.einsum("td,vd->tv", row_block, head, preferred_element_type=jnp.float32)
                / LOGIT_DIVISOR
            )
            highest = jnp.max(logits, axis=1)
            masses = jnp.sum(jnp.exp(logits - highest[:, None]), axis=1)
            chosen = jnp.sum(jnp.where(wanted[:, None] == vocab_ids[None, :], logits, 0.0), axis=1)
            return jnp.stack([highest, masses, chosen])

        stats = lax.map(one_block, jnp.arange(block_count, dtype=jnp.int32))
        return jnp.transpose(stats, (1, 0, 2)).reshape(3, groups, token_count)

    row_span = local_count * CAP
    residual_first, slot_first, outgoing_first = model_entry(0)
    produced_first = model_experts(0, exchange(outgoing_first))
    residual_second, slot_second, outgoing_second = model_entry(1)
    crossed = exchange(jnp.concatenate([produced_first, outgoing_second], axis=1))
    final_first = model_exit(0, residual_first, slot_first, crossed, stride=2 * row_span)
    gathered_first = lax.all_gather(final_first, "exp", axis=0, tiled=True)
    produced_second = model_experts(1, crossed[:, row_span:])
    final_second = model_exit(1, residual_second, slot_second, exchange(produced_second))
    gathered_second = lax.all_gather(final_second, "exp", axis=0, tiled=True)
    stats_first = model_stats(0, gathered_first)
    stats_second = model_stats(1, gathered_second)
    stacked = jnp.transpose(jnp.stack([stats_first, stats_second]), (2, 1, 0, 3))
    gathered = lax.all_to_all(stacked, "exp", 0, 0, tiled=True)
    all_max = gathered[:, 0]
    all_mass = gathered[:, 1]
    all_hit = gathered[:, 2]
    final_max = jnp.max(all_max, axis=0)
    final_mass = jnp.sum(all_mass * jnp.exp(all_max - final_max[None]), axis=0)
    final_hit = jnp.sum(all_hit, axis=0)
    token_logp = final_hit - (final_max + jnp.log(final_mass))
    difference = token_logp[0] - token_logp[1]
    seq_sums = jnp.sum(member.astype(jnp.float32) * difference[:, None], axis=0)
    devices = lax.axis_size("req") * lax.axis_size("exp")
    per_device_seqs = seq_sums.shape[0]
    everyone = devices * per_device_seqs
    dense_totals = jnp.sum(
        (owners[:, None] == jnp.arange(everyone, dtype=jnp.int32)[None, :]).astype(jnp.float32)
        * seq_sums[:, None],
        axis=0,
    )
    delivered = lax.all_to_all(
        dense_totals.reshape(devices, per_device_seqs), ("req", "exp"), 0, 0, tiled=True
    )
    seq_totals = jnp.sum(delivered, axis=0)
    return (token_logp, seq_totals)


def solution(mesh):
    in_specs = (
        P(None, ("req", "exp"), None),
        P(("req", "exp"), None),
        P("req"),
        P(None, ("req", "exp"), None),
        P(None, ("req", "exp"), None),
        P(("req", "exp")),
        P(),
        P(),
        P(),
        P(None, "exp", None, None),
        P(None, "exp", None, None),
        P(None, "exp", None),
    )
    out_specs = (P(None, ("req", "exp")), P(("req", "exp")))
    return jax.shard_map(
        per_device, mesh=mesh, in_specs=in_specs, out_specs=out_specs, check_vma=False
    )
```
